32 devices in a mesh: seq: 8 (over y, x, core), rep: 4 (over z).
Axes of the slice: x: 2, y: 2, z: 4, core: 2. Of those that a mesh axis runs over, the one named last changes fastest.
Arguments:
- out_grad: bfloat16 [4, 16, 131072], P('rep', None, 'seq'), may hold values from -6 to 6
- gate_act: bfloat16 [4, 16, 131072], P('rep', None, 'seq'), may hold values from -6 to 6
- conv_out: bfloat16 [4, 16, 131072], P('rep', None, 'seq'), may hold values from -6 to 6
- value_act: bfloat16 [4, 16, 131072], P('rep', None, 'seq'), may hold values from -6 to 6
- filter_taps: float32 [131072], P('seq'), may hold values from -1 to 1
- skip_gain: float32 [16], replicated, may hold values from 0.25 to 1.75
Outputs:
- gate_grad: bfloat16 [4, 16, 131072], P('rep', None, 'seq')
- value_grad: bfloat16 [4, 16, 131072], P('rep', None, 'seq')
- filter_grad: float32 [131072], P('seq')
The draws below stay inside these ranges and needn't reach their ends.
All inputs are finite; a program needn't handle non-finite values.
Results may differ from the reference program's by a relative error of at most 0.001.
Values sent between devices are 32-bit elements; how exact they have to be, the bound alone decides.
No kernel may reach another device: no remote copies, remote signals or barrier semaphores. Data moves between devices by JAX's collectives and lax.ppermute only.
A program may use at most 128 MiB of HBM per device.

```python
import math
import jax
import jax.numpy as jnp
from jax import lax

CH = 16
LENGTH = 131072
SEQS = 4


def draw_filter_taps(key, part):
    key_rough, key_level = jax.random.split(jax.random.fold_in(key, 11), 2)
    positions = jnp.arange(LENGTH).astype(jnp.float32)
    rough_part = jnp.clip(jax.random.normal(key_rough, (LENGTH,), jnp.float32), -4.0, 4.0)
    level_mult = jax.random.uniform(key_level, (LENGTH,), jnp.float32, 0.5, 1.5)
    envelope = 0.4 + 0.6 * jnp.exp(-positions * (3.0 / LENGTH))
    values = rough_part * level_mult * envelope
    return (values * (1.0 / math.sqrt(LENGTH))).astype(jnp.float32)


def steps_of(rng, shape, pieces, least, top_value):
    gain = 1.0
    for axis_at, shards_of in pieces:
        steps = jax.random.uniform(jax.random.fold_in(jax.random.fold_in(rng, 6), axis_at), (shards_of,), jnp.float32, least / len(pieces), top_value / len(pieces))
        gain = gain * jnp.repeat(jnp.exp(steps), shape[axis_at] // shards_of).reshape((-1,) + (1,) * (len(shape) - 1 - axis_at))
    return gain


def scatter_about(key, extent, width, limit, cuts=(), kind=jnp.bfloat16):
    array = jax.random.normal(key, extent, jnp.float32) * width
    if len(cuts) > 0:
        array = steps_of(key, extent, cuts, -0.22, 0.18) * array
    return jnp.clip(array, min=-limit, max=limit).astype(kind)


def setup_inputs(seed: int = 0) -> dict:
    keys = jax.random.split(jax.random.key(seed), 7)
    out_grad = scatter_about(keys[0], (SEQS, CH, LENGTH), 1.0, 6.0, ((0, 4), (2, 8)))
    gate_act = scatter_about(keys[1], (SEQS, CH, LENGTH), 1.0, 6.0, ((0, 4), (2, 8)))
    conv_out = scatter_about(keys[2], (SEQS, CH, LENGTH), 1.0, 6.0, ((0, 4), (2, 8)))
    value_act = scatter_about(keys[3], (SEQS, CH, LENGTH), 1.0, 6.0, ((0, 4), (2, 8)))
    filter_taps = draw_filter_taps(jax.random.fold_in(keys[6], 71), 0)
    skip_gain = jnp.clip(1.0 + 0.15 * jax.random.normal(keys[5], (CH,), jnp.float32), 0.25, 1.75)
    return dict(out_grad=out_grad, gate_act=gate_act, conv_out=conv_out, value_act=value_act, filter_taps=filter_taps, skip_gain=skip_gain)


def reference(out_grad, gate_act, conv_out, value_act, filter_taps, skip_gain):
    points = 2 * LENGTH
    filter_spec = jnp.fft.rfft(filter_taps.astype(jnp.float32), n=points)

    def per_sequence(seq_rows):
        grad_rows, gate_rows, value_rows = seq_rows
        gated_rows = grad_rows.astype(jnp.float32) * gate_rows.astype(jnp.float32)
        gated_spec = jnp.fft.rfft(gated_rows, n=points, axis=-1)
        value_spec = jnp.fft.rfft(value_rows.astype(jnp.float32), n=points, axis=-1)
        carried = jnp.fft.irfft(jnp.conj(filter_spec)[None, :] * gated_spec, n=points, axis=-1)[:, :LENGTH]
        value_grad = (carried + skip_gain[:, None] * gated_rows).astype(jnp.bfloat16)
        lag_spec = lax.optimization_barrier(jnp.sum(gated_spec * jnp.conj(value_spec), axis=0))
        lag_sums = jnp.fft.irfft(lag_spec, n=points)[:LENGTH]
        return (value_grad, lag_sums)
    value_grad, lag_sums = lax.map(per_sequence, (out_grad, gate_act, value_act))
    gate_grad = (out_grad.astype(jnp.float32) * conv_out.astype(jnp.float32)).astype(jnp.bfloat16)
    filter_grad = lax.optimization_barrier(jnp.sum(lag_sums, axis=0)) * (1.0 / math.sqrt(SEQS * CH * LENGTH))
    return (gate_grad, value_grad, filter_grad)
```

```python
import math

import jax
import jax.numpy as jnp
from jax import lax
from jax.sharding import PartitionSpec as P

HIGHEST = lax.Precision.HIGHEST
LANES = 128


def unit_table(product, modulus):
    phase_rad = (product % modulus).astype(jnp.float32) * (-2.0 * math.pi / modulus)
    return (jnp.cos(phase_rad), jnp.sin(phase_rad))


def row_order(seq_count):
    slot_ids = jnp.arange(2 * seq_count, dtype=jnp.int32)
    owner_dev = slot_ids // 2
    second = jnp.where(owner_dev == 0, seq_count, 2 * seq_count - owner_dev)
    return jnp.where(slot_ids % 2 == 0, owner_dev, second)


def lmul(table, values):
    return jnp.tensordot(table, values, axes=1, precision=HIGHEST)


def rmul(values, table):
    return jnp.tensordot(values, table, axes=1, precision=HIGHEST)


def swap_leading(values):
    return lax.all_to_all(values, "seq", split_axis=0, concat_axis=0, tiled=True)


def local_inverse(spec_re, spec_im, seq_count, slot_freq, offsets, modulus):
    rows_a = spec_re.shape[0]
    length_s = rows_a * LANES
    quota = spec_re.shape[2]
    sub = length_s // seq_count // LANES
    steps_a = jnp.arange(rows_a, dtype=jnp.int32)
    steps_b = jnp.arange(LANES, dtype=jnp.int32)
    last_re, last_im = unit_table(steps_b[:, None] * steps_b[None, :], LANES)
    u_re = rmul(spec_re, last_re) + rmul(spec_im, last_im)
    u_im = rmul(spec_im, last_re) - rmul(spec_re, last_im)
    tw_re, tw_im = unit_table(steps_a[:, None] * steps_b[None, :], length_s)
    tw_re = tw_re[:, None, None, :]
    tw_im = tw_im[:, None, None, :]
    u_re, u_im = (u_re * tw_re + u_im * tw_im, u_im * tw_re - u_re * tw_im)
    first_re, first_im = unit_table(steps_a[:, None] * steps_a[None, :], rows_a)
    out_re = lmul(first_re, u_re) + lmul(first_im, u_im)
    out_im = lmul(first_re, u_im) - lmul(first_im, u_re)
    both = jnp.stack([out_re, out_im], axis=0).reshape(2, seq_count, sub, 2, quota, LANES)
    recv = swap_leading(both.transpose(1, 3, 0, 2, 4, 5))
    recv = recv.reshape(2 * seq_count, 2, sub, quota, LANES)
    twist_re, twist_im = unit_table(slot_freq[:, None] * offsets[None, :], modulus)
    twist_re = twist_re.reshape(2 * seq_count, sub, 1, LANES)
    twist_im = twist_im.reshape(2 * seq_count, sub, 1, LANES)
    z_re = recv[:, 0]
    z_im = recv[:, 1]
    unt = jnp.stack(
        [z_re * twist_re + z_im * twist_im, z_im * twist_re - z_re * twist_im], axis=1
    )
    sources = jnp.arange(seq_count, dtype=jnp.int32)
    mix_re, mix_im = unit_table(sources[:, None] * slot_freq[None, :], 2 * seq_count)
    mix = jnp.stack([mix_re, mix_im], axis=-1).reshape(seq_count, 4 * seq_count)
    rows_out = lmul(mix, unt.reshape(4 * seq_count, sub, quota, LANES))
    back = swap_leading(rows_out)
    return back.transpose(2, 0, 1, 3).reshape(quota, length_s)


def local(out_grad, gate_act, conv_out, value_act, filter_taps, skip_gain):
    batch_rows = out_grad.shape[0]
    channels = out_grad.shape[1]
    length_s = out_grad.shape[2]
    seq_count = lax.axis_size("seq")
    row_total = batch_rows * channels
    stack_rows = 2 * row_total + 1
    blk = length_s // seq_count
    sub = blk // LANES
    rows_a = length_s // LANES
    modulus = 2 * seq_count * length_s
    slot_freq = row_order(seq_count)
    offsets = lax.axis_index("seq") * blk + jnp.arange(blk, dtype=jnp.int32)

    gated_rows = out_grad.astype(jnp.float32) * gate_act.astype(jnp.float32)
    gate_grad = (out_grad.astype(jnp.float32) * conv_out.astype(jnp.float32)).astype(jnp.bfloat16)
    stacked = jnp.concatenate(
        [
            gated_rows.reshape(row_total, length_s),
            value_act.astype(jnp.float32).reshape(row_total, length_s),
            filter_taps.reshape(1, length_s),
        ],
        axis=0,
    )
    recv1 = swap_leading(stacked.reshape(stack_rows, seq_count, blk).transpose(1, 0, 2))
    sources = jnp.arange(seq_count, dtype=jnp.int32)
    cross_re, cross_im = unit_table(slot_freq[:, None] * sources[None, :], 2 * seq_count)
    mixed = lmul(jnp.concatenate([cross_re, cross_im], axis=0), recv1)
    mixed = mixed.reshape(2, 2 * seq_count, stack_rows, blk)
    twist_re, twist_im = unit_table(slot_freq[:, None] * offsets[None, :], modulus)
    twist_re = twist_re[:, None, :]
    twist_im = twist_im[:, None, :]
    m_re = mixed[0]
    m_im = mixed[1]
    y = jnp.stack(
        [m_re * twist_re - m_im * twist_im, m_re * twist_im + m_im * twist_re], axis=0
    )
    y = y.reshape(2, seq_count, 2, stack_rows, sub, LANES).transpose(1, 4, 0, 2, 3, 5)
    recv2 = swap_leading(y)
    steps_a = jnp.arange(rows_a, dtype=jnp.int32)
    steps_b = jnp.arange(LANES, dtype=jnp.int32)
    first_re, first_im = unit_table(steps_a[:, None] * steps_a[None, :], rows_a)
    block = jnp.stack(
        [
            jnp.stack([first_re, -first_im], axis=-1),
            jnp.stack([first_im, first_re], axis=-1),
        ],
        axis=1,
    ).reshape(2 * rows_a, 2 * rows_a)
    y1 = lmul(block, recv2.reshape(2 * rows_a, 2 * stack_rows * LANES))
    y1 = y1.reshape(rows_a, 2, 2, stack_rows, LANES)
    tw_re, tw_im = unit_table(steps_a[:, None] * steps_b[None, :], length_s)
    tw_re = tw_re[:, None, None, :]
    tw_im = tw_im[:, None, None, :]
    y1_re = y1[:, 0]
    y1_im = y1[:, 1]
    y2_re = y1_re * tw_re - y1_im * tw_im
    y2_im = y1_re * tw_im + y1_im * tw_re
    last_re, last_im = unit_table(steps_b[:, None] * steps_b[None, :], LANES)
    spec_re = rmul(y2_re, last_re) - rmul(y2_im, last_im)
    spec_im = rmul(y2_re, last_im) + rmul(y2_im, last_re)
    grad_re = spec_re[:, :, :row_total]
    grad_im = spec_im[:, :, :row_total]
    value_re = spec_re[:, :, row_total : 2 * row_total]
    value_im = spec_im[:, :, row_total : 2 * row_total]
    filt_re = spec_re[:, :, 2 * row_total :]
    filt_im = spec_im[:, :, 2 * row_total :]
    carry_re = filt_re * grad_re + filt_im * grad_im
    carry_im = filt_re * grad_im - filt_im * grad_re
    lag_re = jnp.sum(grad_re * value_re + grad_im * value_im, axis=2, keepdims=True)
    lag_im = jnp.sum(grad_im * value_re - grad_re * value_im, axis=2, keepdims=True)
    lag_re, lag_im = lax.psum((lag_re, lag_im), "rep")
    rows_time = local_inverse(carry_re, carry_im, seq_count, slot_freq, offsets, modulus)
    lag_time = local_inverse(lag_re, lag_im, seq_count, slot_freq, offsets, modulus)
    inv_points = 1.0 / modulus
    carried = (rows_time * inv_points).reshape(batch_rows, channels, length_s)
    value_grad = (carried + skip_gain[None, :, None] * gated_rows).astype(jnp.bfloat16)
    norm_scale = 1.0 / math.sqrt(
        batch_rows * lax.axis_size("rep") * channels * length_s * seq_count
    )
    filter_grad = lag_time[0] * inv_points * norm_scale
    return (gate_grad, value_grad, filter_grad)


def solution(mesh):
    return jax.shard_map(
        local,
        mesh=mesh,
        in_specs=(
            P("rep", None, "seq"),
            P("rep", None, "seq"),
            P("rep", None, "seq"),
            P("rep", None, "seq"),
            P("seq"),
            P(),
        ),
        out_specs=(P("rep", None, "seq"), P("rep", None, "seq"), P("seq")),
        check_vma=False,
    )
```

```python
import math

import jax
import jax.numpy as jnp
from jax import lax
from jax.sharding import PartitionSpec as P

HIGHEST = lax.Precision.HIGHEST
LANES = 128


def unit_table(product, modulus):
    phase_rad = (product % modulus).astype(jnp.float32) * (-2.0 * math.pi / modulus)
    return (jnp.cos(phase_rad), jnp.sin(phase_rad))


def row_order(seq_count):
    slot_ids = jnp.arange(2 * seq_count, dtype=jnp.int32)
    owner_dev = slot_ids // 2
    second = jnp.where(owner_dev == 0, seq_count, 2 * seq_count - owner_dev)
    return jnp.where(slot_ids % 2 == 0, owner_dev, second)


def lmul(table, values):
    return jnp.tensordot(table, values, axes=1, precision=HIGHEST)


def rmul(values, table):
    return jnp.tensordot(values, table, axes=1, precision=HIGHEST)


def swap_leading(values):
    return lax.all_to_all(values, "seq", split_axis=0, concat_axis=0, tiled=True)


def local_inverse(spec_re, spec_im, seq_count, slot_freq, offsets, modulus):
    rows_a = spec_re.shape[0]
    length_s = rows_a * LANES
    quota = spec_re.shape[2]
    sub = length_s // seq_count // LANES
    steps_a = jnp.arange(rows_a, dtype=jnp.int32)
    steps_b = jnp.arange(LANES, dtype=jnp.int32)
    last_re, last_im = unit_table(steps_b[:, None] * steps_b[None, :], LANES)
    u_re = rmul(spec_re, last_re) + rmul(spec_im, last_im)
    u_im = rmul(spec_im, last_re) - rmul(spec_re, last_im)
    tw_re, tw_im = unit_table(steps_a[:, None] * steps_b[None, :], length_s)
    tw_re = tw_re[:, None, None, :]
    tw_im = tw_im[:, None, None, :]
    u_re, u_im = (u_re * tw_re + u_im * tw_im, u_im * tw_re - u_re * tw_im)
    first_re, first_im = unit_table(steps_a[:, None] * steps_a[None, :], rows_a)
    out_re = lmul(first_re, u_re) + lmul(first_im, u_im)
    out_im = lmul(first_re, u_im) - lmul(first_im, u_re)
    dev = lax.axis_index("seq")
    is_first = dev == 0
    own_freq = (dev, jnp.where(is_first, seq_count, 2 * seq_count - dev))
    all_offsets = jnp.arange(length_s, dtype=jnp.int32)
    untwisted = []
    for p in range(2):
        twist_re, twist_im = unit_table(own_freq[p] * all_offsets, modulus)
        twist_re = twist_re.reshape(rows_a, 1, LANES)
        twist_im = twist_im.reshape(rows_a, 1, LANES)
        z_re = out_re[:, p]
        z_im = out_im[:, p]
        untwisted.append(
            (z_re * twist_re + z_im * twist_im, z_im * twist_re - z_re * twist_im)
        )
    send_a = untwisted[0][0]
    send_b = jnp.where(is_first, untwisted[1][0], untwisted[0][1])
    both = jnp.stack([send_a, send_b], axis=0).reshape(2, seq_count, sub, quota, LANES)
    recv = swap_leading(both.transpose(1, 0, 2, 3, 4))
    sources = jnp.arange(seq_count, dtype=jnp.int32)
    mix_re, mix_im = unit_table(sources[:, None] * sources[None, :], 2 * seq_count)
    half_re, _ = unit_table(sources * seq_count, 2 * seq_count)
    first_src = (sources == 0)[None, :]
    mix = jnp.stack(
        [
            jnp.where(first_src, 1.0, 2.0 * mix_re),
            jnp.where(first_src, half_re[:, None], 2.0 * mix_im),
        ],
        axis=-1,
    ).reshape(seq_count, 2 * seq_count)
    rows_out = lmul(mix, recv.reshape(2 * seq_count, sub, quota, LANES))
    back = swap_leading(rows_out)
    return back.transpose(2, 0, 1, 3).reshape(quota, length_s)


def local(out_grad, gate_act, conv_out, value_act, filter_taps, skip_gain):
    batch_rows = out_grad.shape[0]
    channels = out_grad.shape[1]
    length_s = out_grad.shape[2]
    seq_count = lax.axis_size("seq")
    row_total = batch_rows * channels
    stack_rows = 2 * row_total + 1
    blk = length_s // seq_count
    sub = blk // LANES
    rows_a = length_s // LANES
    modulus = 2 * seq_count * length_s
    slot_freq = row_order(seq_count)
    offsets = lax.axis_index("seq") * blk + jnp.arange(blk, dtype=jnp.int32)

    gated_rows = out_grad.astype(jnp.float32) * gate_act.astype(jnp.float32)
    gate_grad = (out_grad.astype(jnp.float32) * conv_out.astype(jnp.float32)).astype(jnp.bfloat16)
    stacked = jnp.concatenate(
        [
            gated_rows.reshape(row_total, length_s),
            value_act.astype(jnp.float32).reshape(row_total, length_s),
            filter_taps.reshape(1, length_s),
        ],
        axis=0,
    )
    recv1 = swap_leading(stacked.reshape(stack_rows, seq_count, blk).transpose(1, 0, 2))
    sources = jnp.arange(seq_count, dtype=jnp.int32)
    cross_re, cross_im = unit_table(sources[:, None] * sources[None, :], 2 * seq_count)
    half_re, _ = unit_table(sources * seq_count, 2 * seq_count)
    cross = jnp.stack(
        [cross_re, jnp.where((sources == 0)[:, None], half_re[None, :], cross_im)], axis=1
    ).reshape(2 * seq_count, seq_count)
    mixed = lmul(cross, recv1).reshape(seq_count, 2, stack_rows, sub, LANES)
    recv2 = swap_leading(mixed.transpose(0, 3, 1, 2, 4))
    dev = lax.axis_index("seq")
    is_first = dev == 0
    own_freq = (dev, jnp.where(is_first, seq_count, 2 * seq_count - dev))
    keep_im = jnp.where(is_first, 0.0, 1.0)
    part_a = recv2[:, :, 0]
    part_b = recv2[:, :, 1]
    rebuilt = (
        (part_a, part_b * keep_im),
        (jnp.where(is_first, part_b, part_a), -part_b * keep_im),
    )
    all_offsets = jnp.arange(length_s, dtype=jnp.int32)
    twisted_re = []
    twisted_im = []
    for p in range(2):
        twist_re, twist_im = unit_table(own_freq[p] * all_offsets, modulus)
        twist_re = twist_re.reshape(seq_count, sub, 1, LANES)
        twist_im = twist_im.reshape(seq_count, sub, 1, LANES)
        m_re, m_im = rebuilt[p]
        twisted_re.append(m_re * twist_re - m_im * twist_im)
        twisted_im.append(m_re * twist_im + m_im * twist_re)
    recv2 = jnp.stack(
        [jnp.stack(twisted_re, axis=2), jnp.stack(twisted_im, axis=2)], axis=2
    )
    steps_a = jnp.arange(rows_a, dtype=jnp.int32)
    steps_b = jnp.arange(LANES, dtype=jnp.int32)
    first_re, first_im = unit_table(steps_a[:, None] * steps_a[None, :], rows_a)
    block = jnp.stack(
        [
            jnp.stack([first_re, -first_im], axis=-1),
            jnp.stack([first_im, first_re], axis=-1),
        ],
        axis=1,
    ).reshape(2 * rows_a, 2 * rows_a)
    y1 = lmul(block, recv2.reshape(2 * rows_a, 2 * stack_rows * LANES))
    y1 = y1.reshape(rows_a, 2, 2, stack_rows, LANES)
    tw_re, tw_im = unit_table(steps_a[:, None] * steps_b[None, :], length_s)
    tw_re = tw_re[:, None, None, :]
    tw_im = tw_im[:, None, None, :]
    y1_re = y1[:, 0]
    y1_im = y1[:, 1]
    y2_re = y1_re * tw_re - y1_im * tw_im
    y2_im = y1_re * tw_im + y1_im * tw_re
    last_re, last_im = unit_table(steps_b[:, None] * steps_b[None, :], LANES)
    spec_re = rmul(y2_re, last_re) - rmul(y2_im, last_im)
    spec_im = rmul(y2_re, last_im) + rmul(y2_im, last_re)
    grad_re = spec_re[:, :, :row_total]
    grad_im = spec_im[:, :, :row_total]
    value_re = spec_re[:, :, row_total : 2 * row_total]
    value_im = spec_im[:, :, row_total : 2 * row_total]
    filt_re = spec_re[:, :, 2 * row_total :]
    filt_im = spec_im[:, :, 2 * row_total :]
    carry_re = filt_re * grad_re + filt_im * grad_im
    carry_im = filt_re * grad_im - filt_im * grad_re
    lag_re = jnp.sum(grad_re * value_re + grad_im * value_im, axis=2, keepdims=True)
    lag_im = jnp.sum(grad_im * value_re - grad_re * value_im, axis=2, keepdims=True)
    lag_re, lag_im = lax.psum((lag_re, lag_im), "rep")
    rows_time = local_inverse(carry_re, carry_im, seq_count, slot_freq, offsets, modulus)
    lag_time = local_inverse(lag_re, lag_im, seq_count, slot_freq, offsets, modulus)
    inv_points = 1.0 / modulus
    carried = (rows_time * inv_points).reshape(batch_rows, channels, length_s)
    value_grad = (carried + skip_gain[None, :, None] * gated_rows).astype(jnp.bfloat16)
    norm_scale = 1.0 / math.sqrt(
        batch_rows * lax.axis_size("rep") * channels * length_s * seq_count
    )
    filter_grad = lag_time[0] * inv_points * norm_scale
    return (gate_grad, value_grad, filter_grad)


def solution(mesh):
    return jax.shard_map(
        local,
        mesh=mesh,
        in_specs=(
            P("rep", None, "seq"),
            P("rep", None, "seq"),
            P("rep", None, "seq"),
            P("rep", None, "seq"),
            P("seq"),
            P(),
        ),
        out_specs=(P("rep", None, "seq"), P("rep", None, "seq"), P("seq")),
        check_vma=False,
    )
```

```python
import math

import jax
import jax.numpy as jnp
from jax import lax
from jax.sharding import PartitionSpec as P

HIGHEST = lax.Precision.HIGHEST
LANES = 128


def unit_table(product, modulus):
    phase_rad = (product % modulus).astype(jnp.float32) * (-2.0 * math.pi / modulus)
    return (jnp.cos(phase_rad), jnp.sin(phase_rad))


def row_order(seq_count):
    slot_ids = jnp.arange(2 * seq_count, dtype=jnp.int32)
    owner_dev = slot_ids // 2
    second = jnp.where(owner_dev == 0, seq_count, 2 * seq_count - owner_dev)
    return jnp.where(slot_ids % 2 == 0, owner_dev, second)


def lmul(table, values):
    return jnp.tensordot(table, values, axes=1, precision=HIGHEST)


def rmul(values, table):
    return jnp.tensordot(values, table, axes=1, precision=HIGHEST)


def swap_leading(values):
    return lax.all_to_all(values, "seq", split_axis=0, concat_axis=0, tiled=True)


def rep_sum(*values):
    count = lax.axis_size("rep")
    if count & (count - 1):
        return lax.psum(values, "rep")
    dist = 1
    while dist < count:
        perm = [(i, i ^ dist) for i in range(count)]
        values = tuple(v + lax.ppermute(v, "rep", perm) for v in values)
        dist *= 2
    return values


def local_inverse(spec_re, spec_im, seq_count, slot_freq, offsets, modulus):
    rows_a = spec_re.shape[0]
    length_s = rows_a * LANES
    quota = spec_re.shape[2]
    sub = length_s // seq_count // LANES
    steps_a = jnp.arange(rows_a, dtype=jnp.int32)
    steps_b = jnp.arange(LANES, dtype=jnp.int32)
    last_re, last_im = unit_table(steps_b[:, None] * steps_b[None, :], LANES)
    u_re = rmul(spec_re, last_re) + rmul(spec_im, last_im)
    u_im = rmul(spec_im, last_re) - rmul(spec_re, last_im)
    tw_re, tw_im = unit_table(steps_a[:, None] * steps_b[None, :], length_s)
    tw_re = tw_re[:, None, None, :]
    tw_im = tw_im[:, None, None, :]
    u_re, u_im = (u_re * tw_re + u_im * tw_im, u_im * tw_re - u_re * tw_im)
    first_re, first_im = unit_table(steps_a[:, None] * steps_a[None, :], rows_a)
    out_re = lmul(first_re, u_re) + lmul(first_im, u_im)
    out_im = lmul(first_re, u_im) - lmul(first_im, u_re)
    dev = lax.axis_index("seq")
    is_first = dev == 0
    own_freq = (dev, jnp.where(is_first, seq_count, 2 * seq_count - dev))
    all_offsets = jnp.arange(length_s, dtype=jnp.int32)
    untwisted = []
    for p in range(2):
        twist_re, twist_im = unit_table(own_freq[p] * all_offsets, modulus)
        twist_re = twist_re.reshape(rows_a, 1, LANES)
        twist_im = twist_im.reshape(rows_a, 1, LANES)
        z_re = out_re[:, p]
        z_im = out_im[:, p]
        untwisted.append(
            (z_re * twist_re + z_im * twist_im, z_im * twist_re - z_re * twist_im)
        )
    send_a = untwisted[0][0]
    send_b = jnp.where(is_first, untwisted[1][0], untwisted[0][1])
    both = jnp.stack([send_a, send_b], axis=0).reshape(2, seq_count, sub, quota, LANES)
    recv = swap_leading(both.transpose(1, 0, 2, 3, 4))
    sources = jnp.arange(seq_count, dtype=jnp.int32)
    mix_re, mix_im = unit_table(sources[:, None] * sources[None, :], 2 * seq_count)
    half_re, _ = unit_table(sources * seq_count, 2 * seq_count)
    first_src = (sources == 0)[None, :]
    mix = jnp.stack(
        [
            jnp.where(first_src, 1.0, 2.0 * mix_re),
            jnp.where(first_src, half_re[:, None], 2.0 * mix_im),
        ],
        axis=-1,
    ).reshape(seq_count, 2 * seq_count)
    rows_out = lmul(mix, recv.reshape(2 * seq_count, sub, quota, LANES))
    back = swap_leading(rows_out)
    return back.transpose(2, 0, 1, 3).reshape(quota, length_s)


def local(out_grad, gate_act, conv_out, value_act, filter_taps, skip_gain):
    batch_rows = out_grad.shape[0]
    channels = out_grad.shape[1]
    length_s = out_grad.shape[2]
    seq_count = lax.axis_size("seq")
    row_total = batch_rows * channels
    stack_rows = 2 * row_total + 1
    blk = length_s // seq_count
    sub = blk // LANES
    rows_a = length_s // LANES
    modulus = 2 * seq_count * length_s
    slot_freq = row_order(seq_count)
    offsets = lax.axis_index("seq") * blk + jnp.arange(blk, dtype=jnp.int32)

    gated_rows = out_grad.astype(jnp.float32) * gate_act.astype(jnp.float32)
    gate_grad = (out_grad.astype(jnp.float32) * conv_out.astype(jnp.float32)).astype(jnp.bfloat16)
    stacked = jnp.concatenate(
        [
            gated_rows.reshape(row_total, length_s),
            value_act.astype(jnp.float32).reshape(row_total, length_s),
            filter_taps.reshape(1, length_s),
        ],
        axis=0,
    )
    recv1 = swap_leading(stacked.reshape(stack_rows, seq_count, blk).transpose(1, 0, 2))
    sources = jnp.arange(seq_count, dtype=jnp.int32)
    cross_re, cross_im = unit_table(sources[:, None] * sources[None, :], 2 * seq_count)
    half_re, _ = unit_table(sources * seq_count, 2 * seq_count)
    cross = jnp.stack(
        [cross_re, jnp.where((sources == 0)[:, None], half_re[None, :], cross_im)], axis=1
    ).reshape(2 * seq_count, seq_count)
    mixed = lmul(cross, recv1).reshape(seq_count, 2, stack_rows, sub, LANES)
    recv2 = swap_leading(mixed.transpose(0, 3, 1, 2, 4))
    dev = lax.axis_index("seq")
    is_first = dev == 0
    own_freq = (dev, jnp.where(is_first, seq_count, 2 * seq_count - dev))
    keep_im = jnp.where(is_first, 0.0, 1.0)
    coef = (
        ((1.0, 0.0), (0.0, keep_im)),
        ((keep_im, 0.0), (1.0 - keep_im, -keep_im)),
    )
    steps_a = jnp.arange(rows_a, dtype=jnp.int32)
    steps_b = jnp.arange(LANES, dtype=jnp.int32)
    lane_step = modulus // LANES
    parts = []
    for p in range(2):
        phase = (steps_a[:, None] * steps_a[None, :]) % LANES * lane_step + (
            LANES * own_freq[p] * steps_a[None, :]
        )
        t_re, t_im = unit_table(phase, modulus)
        for c in range(2):
            cols = []
            for q in range(2):
                k_re, k_im = coef[p][q]
                if c == 0:
                    cols.append(t_re * k_re - t_im * k_im)
                else:
                    cols.append(t_re * k_im + t_im * k_re)
            parts.append(jnp.stack(cols, axis=-1))
    block = jnp.stack(parts, axis=1).reshape(4 * rows_a, 2 * rows_a)
    y1 = lmul(block, recv2.reshape(2 * rows_a, stack_rows * LANES))
    y1 = y1.reshape(rows_a, 2, 2, stack_rows, LANES)
    y2_re = []
    y2_im = []
    for p in range(2):
        phase = steps_b[None, :] * own_freq[p] + steps_a[:, None] * steps_b[None, :] * (
            2 * seq_count
        )
        tw_re, tw_im = unit_table(phase, modulus)
        tw_re = tw_re[:, None, :]
        tw_im = tw_im[:, None, :]
        y1_re = y1[:, p, 0]
        y1_im = y1[:, p, 1]
        y2_re.append(y1_re * tw_re - y1_im * tw_im)
        y2_im.append(y1_re * tw_im + y1_im * tw_re)
    y2_re = jnp.stack(y2_re, axis=1)
    y2_im = jnp.stack(y2_im, axis=1)
    last_re, last_im = unit_table(steps_b[:, None] * steps_b[None, :], LANES)
    spec_re = rmul(y2_re, last_re) - rmul(y2_im, last_im)
    spec_im = rmul(y2_re, last_im) + rmul(y2_im, last_re)
    grad_re = spec_re[:, :, :row_total]
    grad_im = spec_im[:, :, :row_total]
    value_re = spec_re[:, :, row_total : 2 * row_total]
    value_im = spec_im[:, :, row_total : 2 * row_total]
    filt_re = spec_re[:, :, 2 * row_total :]
    filt_im = spec_im[:, :, 2 * row_total :]
    carry_re = filt_re * grad_re + filt_im * grad_im
    carry_im = filt_re * grad_im - filt_im * grad_re
    lag_re = jnp.sum(grad_re * value_re + grad_im * value_im, axis=2, keepdims=True)
    lag_im = jnp.sum(grad_im * value_re - grad_re * value_im, axis=2, keepdims=True)
    lag_re, lag_im = rep_sum(lag_re, lag_im)
    rows_time = local_inverse(carry_re, carry_im, seq_count, slot_freq, offsets, modulus)
    lag_time = local_inverse(lag_re, lag_im, seq_count, slot_freq, offsets, modulus)
    inv_points = 1.0 / modulus
    carried = (rows_time * inv_points).reshape(batch_rows, channels, length_s)
    value_grad = (carried + skip_gain[None, :, None] * gated_rows).astype(jnp.bfloat16)
    norm_scale = 1.0 / math.sqrt(
        batch_rows * lax.axis_size("rep") * channels * length_s * seq_count
    )
    filter_grad = lag_time[0] * inv_points * norm_scale
    return (gate_grad, value_grad, filter_grad)


def solution(mesh):
    return jax.shard_map(
        local,
        mesh=mesh,
        in_specs=(
            P("rep", None, "seq"),
            P("rep", None, "seq"),
            P("rep", None, "seq"),
            P("rep", None, "seq"),
            P("seq"),
            P(),
        ),
        out_specs=(P("rep", None, "seq"), P("rep", None, "seq"), P("seq")),
        check_vma=False,
    )
```

```python
import math

import jax
import jax.numpy as jnp
from jax import lax
from jax.sharding import PartitionSpec as P

HIGHEST = lax.Precision.HIGHEST
LANES = 128


def unit_table(product, modulus):
    phase_rad = (product % modulus).astype(jnp.float32) * (-2.0 * math.pi / modulus)
    return (jnp.cos(phase_rad), jnp.sin(phase_rad))


def row_order(seq_count):
    slot_ids = jnp.arange(2 * seq_count, dtype=jnp.int32)
    owner_dev = slot_ids // 2
    second = jnp.where(owner_dev == 0, seq_count, 2 * seq_count - owner_dev)
    return jnp.where(slot_ids % 2 == 0, owner_dev, second)


def lmul(table, values):
    return jnp.tensordot(table, values, axes=1, precision=HIGHEST)


def rmul(values, table):
    return jnp.tensordot(values, table, axes=1, precision=HIGHEST)


def swap_leading(values):
    return lax.all_to_all(values, "seq", split_axis=0, concat_axis=0, tiled=True)


def rep_sum(*values):
    count = lax.axis_size("rep")
    if count & (count - 1):
        return lax.psum(values, "rep")
    dist = 1
    while dist < count:
        perm = [(i, i ^ dist) for i in range(count)]
        values = tuple(v + lax.ppermute(v, "rep", perm) for v in values)
        dist *= 2
    return values


def local_inverse(spec_re, spec_im, seq_count, slot_freq, offsets, modulus):
    rows_a = spec_re.shape[0]
    length_s = rows_a * LANES
    quota = spec_re.shape[2]
    sub = length_s // seq_count // LANES
    steps_a = jnp.arange(rows_a, dtype=jnp.int32)
    steps_b = jnp.arange(LANES, dtype=jnp.int32)
    last_re, last_im = unit_table(steps_b[:, None] * steps_b[None, :], LANES)
    u_re = rmul(spec_re, last_re) + rmul(spec_im, last_im)
    u_im = rmul(spec_im, last_re) - rmul(spec_re, last_im)
    tw_re, tw_im = unit_table(steps_a[:, None] * steps_b[None, :], length_s)
    tw_re = tw_re[:, None, None, :]
    tw_im = tw_im[:, None, None, :]
    u_re, u_im = (u_re * tw_re + u_im * tw_im, u_im * tw_re - u_re * tw_im)
    first_re, first_im = unit_table(steps_a[:, None] * steps_a[None, :], rows_a)
    out_re = lmul(first_re, u_re) + lmul(first_im, u_im)
    out_im = lmul(first_re, u_im) - lmul(first_im, u_re)
    dev = lax.axis_index("seq")
    is_first = dev == 0
    own_freq = (dev, jnp.where(is_first, seq_count, 2 * seq_count - dev))
    all_offsets = jnp.arange(length_s, dtype=jnp.int32)
    untwisted = []
    for p in range(2):
        twist_re, twist_im = unit_table(own_freq[p] * all_offsets, modulus)
        twist_re = twist_re.reshape(rows_a, 1, LANES)
        twist_im = twist_im.reshape(rows_a, 1, LANES)
        z_re = out_re[:, p]
        z_im = out_im[:, p]
        untwisted.append(
            (z_re * twist_re + z_im * twist_im, z_im * twist_re - z_re * twist_im)
        )
    send_a = untwisted[0][0]
    send_b = jnp.where(is_first, untwisted[1][0], untwisted[0][1])
    both = jnp.stack([send_a, send_b], axis=0).reshape(2, seq_count, sub, quota, LANES)
    recv = swap_leading(both.transpose(1, 0, 2, 3, 4))
    sources = jnp.arange(seq_count, dtype=jnp.int32)
    mix_re, mix_im = unit_table(sources[:, None] * sources[None, :], 2 * seq_count)
    half_re, _ = unit_table(sources * seq_count, 2 * seq_count)
    first_src = (sources == 0)[None, :]
    mix = jnp.stack(
        [
            jnp.where(first_src, 1.0, 2.0 * mix_re),
            jnp.where(first_src, half_re[:, None], 2.0 * mix_im),
        ],
        axis=-1,
    ).reshape(seq_count, 2 * seq_count)
    rows_out = lmul(mix, recv.reshape(2 * seq_count, sub, quota, LANES))
    back = swap_leading(rows_out)
    return back.transpose(2, 0, 1, 3).reshape(quota, length_s)


def forward_rows(stacked, seq_count):
    stack_rows, length_s = stacked.shape
    blk = length_s // seq_count
    sub = blk // LANES
    rows_a = length_s // LANES
    modulus = 2 * seq_count * length_s
    recv1 = swap_leading(stacked.reshape(stack_rows, seq_count, blk).transpose(1, 0, 2))
    sources = jnp.arange(seq_count, dtype=jnp.int32)
    cross_re, cross_im = unit_table(sources[:, None] * sources[None, :], 2 * seq_count)
    half_re, _ = unit_table(sources * seq_count, 2 * seq_count)
    cross = jnp.stack(
        [cross_re, jnp.where((sources == 0)[:, None], half_re[None, :], cross_im)], axis=1
    ).reshape(2 * seq_count, seq_count)
    mixed = lmul(cross, recv1).reshape(seq_count, 2, stack_rows, sub, LANES)
    recv2 = swap_leading(mixed.transpose(0, 3, 1, 2, 4))
    dev = lax.axis_index("seq")
    is_first = dev == 0
    own_freq = (dev, jnp.where(is_first, seq_count, 2 * seq_count - dev))
    keep_im = jnp.where(is_first, 0.0, 1.0)
    coef = (
        ((1.0, 0.0), (0.0, keep_im)),
        ((keep_im, 0.0), (1.0 - keep_im, -keep_im)),
    )
    steps_a = jnp.arange(rows_a, dtype=jnp.int32)
    steps_b = jnp.arange(LANES, dtype=jnp.int32)
    lane_step = modulus // LANES
    parts = []
    for p in range(2):
        phase = (steps_a[:, None] * steps_a[None, :]) % LANES * lane_step + (
            LANES * own_freq[p] * steps_a[None, :]
        )
        t_re, t_im = unit_table(phase, modulus)
        for c in range(2):
            cols = []
            for q in range(2):
                k_re, k_im = coef[p][q]
                if c == 0:
                    cols.append(t_re * k_re - t_im * k_im)
                else:
                    cols.append(t_re * k_im + t_im * k_re)
            parts.append(jnp.stack(cols, axis=-1))
    block = jnp.stack(parts, axis=1).reshape(4 * rows_a, 2 * rows_a)
    y1 = lmul(block, recv2.reshape(2 * rows_a, stack_rows * LANES))
    y1 = y1.reshape(rows_a, 2, 2, stack_rows, LANES)
    y2_re = []
    y2_im = []
    for p in range(2):
        phase = steps_b[None, :] * own_freq[p] + steps_a[:, None] * steps_b[None, :] * (
            2 * seq_count
        )
        tw_re, tw_im = unit_table(phase, modulus)
        tw_re = tw_re[:, None, :]
        tw_im = tw_im[:, None, :]
        y1_re = y1[:, p, 0]
        y1_im = y1[:, p, 1]
        y2_re.append(y1_re * tw_re - y1_im * tw_im)
        y2_im.append(y1_re * tw_im + y1_im * tw_re)
    y2_re = jnp.stack(y2_re, axis=1)
    y2_im = jnp.stack(y2_im, axis=1)
    last_re, last_im = unit_table(steps_b[:, None] * steps_b[None, :], LANES)
    spec_re = rmul(y2_re, last_re) - rmul(y2_im, last_im)
    spec_im = rmul(y2_re, last_im) + rmul(y2_im, last_re)
    return (spec_re, spec_im)


def local(out_grad, gate_act, conv_out, value_act, filter_taps, skip_gain):
    batch_rows = out_grad.shape[0]
    channels = out_grad.shape[1]
    length_s = out_grad.shape[2]
    seq_count = lax.axis_size("seq")
    row_total = batch_rows * channels
    stack_rows = 2 * row_total + 1
    blk = length_s // seq_count
    sub = blk // LANES
    rows_a = length_s // LANES
    modulus = 2 * seq_count * length_s
    slot_freq = row_order(seq_count)
    offsets = lax.axis_index("seq") * blk + jnp.arange(blk, dtype=jnp.int32)

    gated_rows = out_grad.astype(jnp.float32) * gate_act.astype(jnp.float32)
    gate_grad = (out_grad.astype(jnp.float32) * conv_out.astype(jnp.float32)).astype(jnp.bfloat16)
    half = row_total // 2
    grad_flat = gated_rows.reshape(row_total, length_s)
    value_flat = value_act.astype(jnp.float32).reshape(row_total, length_s)
    chunks = (
        jnp.concatenate(
            [grad_flat[:half], value_flat[:half], filter_taps.reshape(1, length_s)], axis=0
        ),
        jnp.concatenate([grad_flat[half:], value_flat[half:]], axis=0),
    )
    specs = [forward_rows(chunk, seq_count) for chunk in chunks]
    filt_re = specs[0][0][:, :, 2 * half :]
    filt_im = specs[0][1][:, :, 2 * half :]
    lag_re = 0.0
    lag_im = 0.0
    carried_parts = []
    for spec_re, spec_im in specs:
        count = spec_re.shape[2] // 2
        grad_re = spec_re[:, :, :count]
        grad_im = spec_im[:, :, :count]
        value_re = spec_re[:, :, count : 2 * count]
        value_im = spec_im[:, :, count : 2 * count]
        carry_re = filt_re * grad_re + filt_im * grad_im
        carry_im = filt_re * grad_im - filt_im * grad_re
        lag_re = lag_re + jnp.sum(grad_re * value_re + grad_im * value_im, axis=2, keepdims=True)
        lag_im = lag_im + jnp.sum(grad_im * value_re - grad_re * value_im, axis=2, keepdims=True)
        carried_parts.append(
            local_inverse(carry_re, carry_im, seq_count, slot_freq, offsets, modulus)
        )
    lag_re, lag_im = rep_sum(lag_re, lag_im)
    rows_time = jnp.concatenate(carried_parts, axis=0)
    lag_time = local_inverse(lag_re, lag_im, seq_count, slot_freq, offsets, modulus)
    inv_points = 1.0 / modulus
    carried = (rows_time * inv_points).reshape(batch_rows, channels, length_s)
    value_grad = (carried + skip_gain[None, :, None] * gated_rows).astype(jnp.bfloat16)
    norm_scale = 1.0 / math.sqrt(
        batch_rows * lax.axis_size("rep") * channels * length_s * seq_count
    )
    filter_grad = lag_time[0] * inv_points * norm_scale
    return (gate_grad, value_grad, filter_grad)


def solution(mesh):
    return jax.shard_map(
        local,
        mesh=mesh,
        in_specs=(
            P("rep", None, "seq"),
            P("rep", None, "seq"),
            P("rep", None, "seq"),
            P("rep", None, "seq"),
            P("seq"),
            P(),
        ),
        out_specs=(P("rep", None, "seq"), P("rep", None, "seq"), P("seq")),
        check_vma=False,
    )
```

```python
import math

import jax
import jax.numpy as jnp
from jax import lax
from jax.sharding import PartitionSpec as P

MATMUL_PRECISION = lax.Precision.HIGH
LANES = 128


def unit_table(product, modulus):
    phase_rad = (product % modulus).astype(jnp.float32) * (-2.0 * math.pi / modulus)
    return (jnp.cos(phase_rad), jnp.sin(phase_rad))


def row_order(seq_count):
    slot_ids = jnp.arange(2 * seq_count, dtype=jnp.int32)
    owner_dev = slot_ids // 2
    second = jnp.where(owner_dev == 0, seq_count, 2 * seq_count - owner_dev)
    return jnp.where(slot_ids % 2 == 0, owner_dev, second)


def lmul(table, values):
    return jnp.tensordot(table, values, axes=1, precision=MATMUL_PRECISION)


def rmul(values, table):
    return jnp.tensordot(values, table, axes=1, precision=MATMUL_PRECISION)


def swap_leading(values):
    return lax.all_to_all(values, "seq", split_axis=0, concat_axis=0, tiled=True)


def rep_sum(*values):
    count = lax.axis_size("rep")
    if count & (count - 1):
        return lax.psum(values, "rep")
    dist = 1
    while dist < count:
        perm = [(i, i ^ dist) for i in range(count)]
        values = tuple(v + lax.ppermute(v, "rep", perm) for v in values)
        dist *= 2
    return values


def local_inverse(spec_re, spec_im, seq_count, slot_freq, offsets, modulus):
    rows_a = spec_re.shape[0]
    length_s = rows_a * LANES
    quota = spec_re.shape[2]
    sub = length_s // seq_count // LANES
    steps_a = jnp.arange(rows_a, dtype=jnp.int32)
    steps_b = jnp.arange(LANES, dtype=jnp.int32)
    last_re, last_im = unit_table(steps_b[:, None] * steps_b[None, :], LANES)
    u_re = rmul(spec_re, last_re) + rmul(spec_im, last_im)
    u_im = rmul(spec_im, last_re) - rmul(spec_re, last_im)
    tw_re, tw_im = unit_table(steps_a[:, None] * steps_b[None, :], length_s)
    tw_re = tw_re[:, None, None, :]
    tw_im = tw_im[:, None, None, :]
    u_re, u_im = (u_re * tw_re + u_im * tw_im, u_im * tw_re - u_re * tw_im)
    first_re, first_im = unit_table(steps_a[:, None] * steps_a[None, :], rows_a)
    out_re = lmul(first_re, u_re) + lmul(first_im, u_im)
    out_im = lmul(first_re, u_im) - lmul(first_im, u_re)
    dev = lax.axis_index("seq")
    is_first = dev == 0
    own_freq = (dev, jnp.where(is_first, seq_count, 2 * seq_count - dev))
    all_offsets = jnp.arange(length_s, dtype=jnp.int32)
    untwisted = []
    for p in range(2):
        twist_re, twist_im = unit_table(own_freq[p] * all_offsets, modulus)
        twist_re = twist_re.reshape(rows_a, 1, LANES)
        twist_im = twist_im.reshape(rows_a, 1, LANES)
        z_re = out_re[:, p]
        z_im = out_im[:, p]
        untwisted.append(
            (z_re * twist_re + z_im * twist_im, z_im * twist_re - z_re * twist_im)
        )
    send_a = untwisted[0][0]
    send_b = jnp.where(is_first, untwisted[1][0], untwisted[0][1])
    return (send_a, send_b)


def cross_inverse(send_a, send_b, seq_count):
    rows_a, quota = send_a.shape[:2]
    length_s = rows_a * LANES
    sub = length_s // seq_count // LANES
    both = jnp.stack([send_a, send_b], axis=0).reshape(2, seq_count, sub, quota, LANES)
    recv = swap_leading(both.transpose(1, 0, 2, 3, 4))
    sources = jnp.arange(seq_count, dtype=jnp.int32)
    mix_re, mix_im = unit_table(sources[:, None] * sources[None, :], 2 * seq_count)
    half_re, _ = unit_table(sources * seq_count, 2 * seq_count)
    first_src = (sources == 0)[None, :]
    mix = jnp.stack(
        [
            jnp.where(first_src, 1.0, 2.0 * mix_re),
            jnp.where(first_src, half_re[:, None], 2.0 * mix_im),
        ],
        axis=-1,
    ).reshape(seq_count, 2 * seq_count)
    rows_out = lmul(mix, recv.reshape(2 * seq_count, sub, quota, LANES))
    back = swap_leading(rows_out)
    return back.transpose(2, 0, 1, 3).reshape(quota, length_s)


def local(out_grad, gate_act, conv_out, value_act, filter_taps, skip_gain):
    batch_rows = out_grad.shape[0]
    channels = out_grad.shape[1]
    length_s = out_grad.shape[2]
    seq_count = lax.axis_size("seq")
    row_total = batch_rows * channels
    stack_rows = 2 * row_total + 1
    blk = length_s // seq_count
    sub = blk // LANES
    rows_a = length_s // LANES
    modulus = 2 * seq_count * length_s
    slot_freq = row_order(seq_count)
    offsets = lax.axis_index("seq") * blk + jnp.arange(blk, dtype=jnp.int32)

    gated_rows = out_grad.astype(jnp.float32) * gate_act.astype(jnp.float32)
    gate_grad = (out_grad.astype(jnp.float32) * conv_out.astype(jnp.float32)).astype(jnp.bfloat16)
    stacked = jnp.concatenate(
        [
            gated_rows.reshape(row_total, length_s),
            value_act.astype(jnp.float32).reshape(row_total, length_s),
            filter_taps.reshape(1, length_s),
        ],
        axis=0,
    )
    recv1 = swap_leading(stacked.reshape(stack_rows, seq_count, blk).transpose(1, 0, 2))
    sources = jnp.arange(seq_count, dtype=jnp.int32)
    cross_re, cross_im = unit_table(sources[:, None] * sources[None, :], 2 * seq_count)
    half_re, _ = unit_table(sources * seq_count, 2 * seq_count)
    cross = jnp.stack(
        [cross_re, jnp.where((sources == 0)[:, None], half_re[None, :], cross_im)], axis=1
    ).reshape(2 * seq_count, seq_count)
    mixed = lmul(cross, recv1).reshape(seq_count, 2, stack_rows, sub, LANES)
    recv2 = swap_leading(mixed.transpose(0, 3, 1, 2, 4))
    dev = lax.axis_index("seq")
    is_first = dev == 0
    own_freq = (dev, jnp.where(is_first, seq_count, 2 * seq_count - dev))
    keep_im = jnp.where(is_first, 0.0, 1.0)
    coef = (
        ((1.0, 0.0), (0.0, keep_im)),
        ((keep_im, 0.0), (1.0 - keep_im, -keep_im)),
    )
    steps_a = jnp.arange(rows_a, dtype=jnp.int32)
    steps_b = jnp.arange(LANES, dtype=jnp.int32)
    lane_step = modulus // LANES
    parts = []
    for p in range(2):
        phase = (steps_a[:, None] * steps_a[None, :]) % LANES * lane_step + (
            LANES * own_freq[p] * steps_a[None, :]
        )
        t_re, t_im = unit_table(phase, modulus)
        for c in range(2):
            cols = []
            for q in range(2):
                k_re, k_im = coef[p][q]
                if c == 0:
                    cols.append(t_re * k_re - t_im * k_im)
                else:
                    cols.append(t_re * k_im + t_im * k_re)
            parts.append(jnp.stack(cols, axis=-1))
    block = jnp.stack(parts, axis=1).reshape(4 * rows_a, 2 * rows_a)
    y1 = lmul(block, recv2.reshape(2 * rows_a, stack_rows * LANES))
    y1 = y1.reshape(rows_a, 2, 2, stack_rows, LANES)
    y2_re = []
    y2_im = []
    for p in range(2):
        phase = steps_b[None, :] * own_freq[p] + steps_a[:, None] * steps_b[None, :] * (
            2 * seq_count
        )
        tw_re, tw_im = unit_table(phase, modulus)
        tw_re = tw_re[:, None, :]
        tw_im = tw_im[:, None, :]
        y1_re = y1[:, p, 0]
        y1_im = y1[:, p, 1]
        y2_re.append(y1_re * tw_re - y1_im * tw_im)
        y2_im.append(y1_re * tw_im + y1_im * tw_re)
    y2_re = jnp.stack(y2_re, axis=1)
    y2_im = jnp.stack(y2_im, axis=1)
    last_re, last_im = unit_table(steps_b[:, None] * steps_b[None, :], LANES)
    spec_re = rmul(y2_re, last_re) - rmul(y2_im, last_im)
    spec_im = rmul(y2_re, last_im) + rmul(y2_im, last_re)
    grad_re = spec_re[:, :, :row_total]
    grad_im = spec_im[:, :, :row_total]
    value_re = spec_re[:, :, row_total : 2 * row_total]
    value_im = spec_im[:, :, row_total : 2 * row_total]
    filt_re = spec_re[:, :, 2 * row_total :]
    filt_im = spec_im[:, :, 2 * row_total :]
    carry_re = filt_re * grad_re + filt_im * grad_im
    carry_im = filt_re * grad_im - filt_im * grad_re
    lag_re = jnp.sum(grad_re * value_re + grad_im * value_im, axis=2, keepdims=True)
    lag_im = jnp.sum(grad_im * value_re - grad_re * value_im, axis=2, keepdims=True)
    lag_re, lag_im = rep_sum(lag_re, lag_im)
    carry_a, carry_b = local_inverse(carry_re, carry_im, seq_count, slot_freq, offsets, modulus)
    lag_a, lag_b = local_inverse(lag_re, lag_im, seq_count, slot_freq, offsets, modulus)
    rows_time = cross_inverse(
        jnp.concatenate([carry_a, lag_a], axis=1),
        jnp.concatenate([carry_b, lag_b], axis=1),
        seq_count,
    )
    lag_time = rows_time[row_total:]
    rows_time = rows_time[:row_total]
    inv_points = 1.0 / modulus
    carried = (rows_time * inv_points).reshape(batch_rows, channels, length_s)
    value_grad = (carried + skip_gain[None, :, None] * gated_rows).astype(jnp.bfloat16)
    norm_scale = 1.0 / math.sqrt(
        batch_rows * lax.axis_size("rep") * channels * length_s * seq_count
    )
    filter_grad = lag_time[0] * inv_points * norm_scale
    return (gate_grad, value_grad, filter_grad)


def solution(mesh):
    return jax.shard_map(
        local,
        mesh=mesh,
        in_specs=(
            P("rep", None, "seq"),
            P("rep", None, "seq"),
            P("rep", None, "seq"),
            P("rep", None, "seq"),
            P("seq"),
            P(),
        ),
        out_specs=(P("rep", None, "seq"), P("rep", None, "seq"), P("seq")),
        check_vma=False,
    )
```

```python
import math

import jax
import jax.numpy as jnp
from jax import lax
from jax.sharding import PartitionSpec as P

MATMUL_PRECISION = lax.Precision.HIGH
LANES = 128


def unit_table(product, modulus):
    phase_rad = (product % modulus).astype(jnp.float32) * (-2.0 * math.pi / modulus)
    return (jnp.cos(phase_rad), jnp.sin(phase_rad))


def row_order(seq_count):
    slot_ids = jnp.arange(2 * seq_count, dtype=jnp.int32)
    owner_dev = slot_ids // 2
    second = jnp.where(owner_dev == 0, seq_count, 2 * seq_count - owner_dev)
    return jnp.where(slot_ids % 2 == 0, owner_dev, second)


def lmul(table, values):
    return jnp.tensordot(table, values, axes=1, precision=MATMUL_PRECISION)


def rmul(values, table):
    return jnp.tensordot(values, table, axes=1, precision=MATMUL_PRECISION)


def swap_leading(values):
    return lax.all_to_all(values, "seq", split_axis=0, concat_axis=0, tiled=True)


def rep_sum(*values):
    count = lax.axis_size("rep")
    if count & (count - 1):
        return lax.psum(values, "rep")
    dist = 1
    while dist < count:
        perm = [(i, i ^ dist) for i in range(count)]
        values = tuple(v + lax.ppermute(v, "rep", perm) for v in values)
        dist *= 2
    return values


def local_inverse(spec_re, spec_im, seq_count, slot_freq, offsets, modulus):
    rows_a = spec_re.shape[0]
    length_s = rows_a * LANES
    quota = spec_re.shape[2]
    sub = length_s // seq_count // LANES
    steps_a = jnp.arange(rows_a, dtype=jnp.int32)
    steps_b = jnp.arange(LANES, dtype=jnp.int32)
    last_re, last_im = unit_table(steps_b[:, None] * steps_b[None, :], LANES)
    u_re = rmul(spec_re, last_re) + rmul(spec_im, last_im)
    u_im = rmul(spec_im, last_re) - rmul(spec_re, last_im)
    tw_re, tw_im = unit_table(steps_a[:, None] * steps_b[None, :], length_s)
    tw_re = tw_re[:, None, None, :]
    tw_im = tw_im[:, None, None, :]
    u_re, u_im = (u_re * tw_re + u_im * tw_im, u_im * tw_re - u_re * tw_im)
    first_re, first_im = unit_table(steps_a[:, None] * steps_a[None, :], rows_a)
    out_re = lmul(first_re, u_re) + lmul(first_im, u_im)
    out_im = lmul(first_re, u_im) - lmul(first_im, u_re)
    dev = lax.axis_index("seq")
    is_first = dev == 0
    own_freq = (dev, jnp.where(is_first, seq_count, 2 * seq_count - dev))
    all_offsets = jnp.arange(length_s, dtype=jnp.int32)
    untwisted = []
    for p in range(2):
        twist_re, twist_im = unit_table(own_freq[p] * all_offsets, modulus)
        twist_re = twist_re.reshape(rows_a, 1, LANES)
        twist_im = twist_im.reshape(rows_a, 1, LANES)
        z_re = out_re[:, p]
        z_im = out_im[:, p]
        untwisted.append(
            (z_re * twist_re + z_im * twist_im, z_im * twist_re - z_re * twist_im)
        )
    send_a = untwisted[0][0]
    send_b = jnp.where(is_first, untwisted[1][0], untwisted[0][1])
    return (send_a, send_b)


def cross_inverse(send_a, send_b, seq_count):
    rows_a, quota = send_a.shape[:2]
    length_s = rows_a * LANES
    sub = length_s // seq_count // LANES
    both = jnp.stack([send_a, send_b], axis=0).reshape(2, seq_count, sub, quota, LANES)
    recv = swap_leading(both.transpose(1, 0, 2, 3, 4))
    sources = jnp.arange(seq_count, dtype=jnp.int32)
    mix_re, mix_im = unit_table(sources[:, None] * sources[None, :], 2 * seq_count)
    half_re, _ = unit_table(sources * seq_count, 2 * seq_count)
    first_src = (sources == 0)[None, :]
    mix = jnp.stack(
        [
            jnp.where(first_src, 1.0, 2.0 * mix_re),
            jnp.where(first_src, half_re[:, None], 2.0 * mix_im),
        ],
        axis=-1,
    ).reshape(seq_count, 2 * seq_count)
    rows_out = lmul(mix, recv.reshape(2 * seq_count, sub, quota, LANES))
    back = swap_leading(rows_out)
    return back.transpose(2, 0, 1, 3).reshape(quota, length_s)


def local(out_grad, gate_act, conv_out, value_act, filter_taps, skip_gain):
    batch_rows = out_grad.shape[0]
    channels = out_grad.shape[1]
    length_s = out_grad.shape[2]
    seq_count = lax.axis_size("seq")
    row_total = batch_rows * channels
    stack_rows = 2 * row_total + 1
    blk = length_s // seq_count
    sub = blk // LANES
    rows_a = length_s // LANES
    modulus = 2 * seq_count * length_s
    slot_freq = row_order(seq_count)
    offsets = lax.axis_index("seq") * blk + jnp.arange(blk, dtype=jnp.int32)

    gated_rows = out_grad.astype(jnp.float32) * gate_act.astype(jnp.float32)
    gate_grad = (out_grad.astype(jnp.float32) * conv_out.astype(jnp.float32)).astype(jnp.bfloat16)
    stacked = jnp.concatenate(
        [
            gated_rows.reshape(row_total, length_s),
            value_act.astype(jnp.float32).reshape(row_total, length_s),
            filter_taps.reshape(1, length_s),
        ],
        axis=0,
    )
    recv1 = swap_leading(stacked.reshape(stack_rows, seq_count, blk).transpose(1, 0, 2))
    sources = jnp.arange(seq_count, dtype=jnp.int32)
    cross_re, cross_im = unit_table(sources[:, None] * sources[None, :], 2 * seq_count)
    half_re, _ = unit_table(sources * seq_count, 2 * seq_count)
    cross = jnp.stack(
        [cross_re, jnp.where((sources == 0)[:, None], half_re[None, :], cross_im)], axis=1
    ).reshape(2 * seq_count, seq_count)
    mixed = lmul(cross, recv1).reshape(seq_count, 2, stack_rows, sub, LANES)
    recv2 = swap_leading(mixed.transpose(0, 3, 1, 2, 4))
    dev = lax.axis_index("seq")
    is_first = dev == 0
    own_freq = (dev, jnp.where(is_first, seq_count, 2 * seq_count - dev))
    keep_im = jnp.where(is_first, 0.0, 1.0)
    coef = (
        ((1.0, 0.0), (0.0, keep_im)),
        ((keep_im, 0.0), (1.0 - keep_im, -keep_im)),
    )
    steps_a = jnp.arange(rows_a, dtype=jnp.int32)
    steps_b = jnp.arange(LANES, dtype=jnp.int32)
    lane_step = modulus // LANES
    parts = []
    for p in range(2):
        phase = (steps_a[:, None] * steps_a[None, :]) % LANES * lane_step + (
            LANES * own_freq[p] * steps_a[None, :]
        )
        t_re, t_im = unit_table(phase, modulus)
        for c in range(2):
            cols = []
            for q in range(2):
                k_re, k_im = coef[p][q]
                if c == 0:
                    cols.append(t_re * k_re - t_im * k_im)
                else:
                    cols.append(t_re * k_im + t_im * k_re)
            parts.append(jnp.stack(cols, axis=-1))
    block = jnp.stack(parts, axis=1).reshape(4 * rows_a, 2 * rows_a)
    y1 = lmul(block, recv2.reshape(2 * rows_a, stack_rows * LANES))
    y1 = y1.reshape(rows_a, 2, 2, stack_rows, LANES)
    y2_re = []
    y2_im = []
    for p in range(2):
        phase = steps_b[None, :] * own_freq[p] + steps_a[:, None] * steps_b[None, :] * (
            2 * seq_count
        )
        tw_re, tw_im = unit_table(phase, modulus)
        tw_re = tw_re[:, None, :]
        tw_im = tw_im[:, None, :]
        y1_re = y1[:, p, 0]
        y1_im = y1[:, p, 1]
        y2_re.append(y1_re * tw_re - y1_im * tw_im)
        y2_im.append(y1_re * tw_im + y1_im * tw_re)
    y2_re = jnp.stack(y2_re, axis=1)
    y2_im = jnp.stack(y2_im, axis=1)
    last_re, last_im = unit_table(steps_b[:, None] * steps_b[None, :], LANES)
    spec_re = rmul(y2_re, last_re) - rmul(y2_im, last_im)
    spec_im = rmul(y2_re, last_im) + rmul(y2_im, last_re)
    grad_re = spec_re[:, :, :row_total]
    grad_im = spec_im[:, :, :row_total]
    value_re = spec_re[:, :, row_total : 2 * row_total]
    value_im = spec_im[:, :, row_total : 2 * row_total]
    filt_re = spec_re[:, :, 2 * row_total :]
    filt_im = spec_im[:, :, 2 * row_total :]
    carry_re = filt_re * grad_re + filt_im * grad_im
    carry_im = filt_re * grad_im - filt_im * grad_re
    lag_re = jnp.sum(grad_re * value_re + grad_im * value_im, axis=2, keepdims=True)
    lag_im = jnp.sum(grad_im * value_re - grad_re * value_im, axis=2, keepdims=True)
    rows_time = cross_inverse(
        *local_inverse(
            jnp.concatenate([carry_re, lag_re], axis=2),
            jnp.concatenate([carry_im, lag_im], axis=2),
            seq_count,
            slot_freq,
            offsets,
            modulus,
        ),
        seq_count,
    )
    (lag_time,) = rep_sum(rows_time[row_total:])
    rows_time = rows_time[:row_total]
    inv_points = 1.0 / modulus
    carried = (rows_time * inv_points).reshape(batch_rows, channels, length_s)
    value_grad = (carried + skip_gain[None, :, None] * gated_rows).astype(jnp.bfloat16)
    norm_scale = 1.0 / math.sqrt(
        batch_rows * lax.axis_size("rep") * channels * length_s * seq_count
    )
    filter_grad = lag_time[0] * inv_points * norm_scale
    return (gate_grad, value_grad, filter_grad)


def solution(mesh):
    return jax.shard_map(
        local,
        mesh=mesh,
        in_specs=(
            P("rep", None, "seq"),
            P("rep", None, "seq"),
            P("rep", None, "seq"),
            P("rep", None, "seq"),
            P("seq"),
            P(),
        ),
        out_specs=(P("rep", None, "seq"), P("rep", None, "seq"), P("seq")),
        check_vma=False,
    )
```

```python
import math

import jax
import jax.numpy as jnp
from jax import lax
from jax.sharding import PartitionSpec as P

MATMUL_PRECISION = lax.Precision.HIGH
LANES = 128


def unit_table(product, modulus):
    phase_rad = (product % modulus).astype(jnp.float32) * (-2.0 * math.pi / modulus)
    return (jnp.cos(phase_rad), jnp.sin(phase_rad))


def row_order(seq_count):
    slot_ids = jnp.arange(2 * seq_count, dtype=jnp.int32)
    owner_dev = slot_ids // 2
    second = jnp.where(owner_dev == 0, seq_count, 2 * seq_count - owner_dev)
    return jnp.where(slot_ids % 2 == 0, owner_dev, second)


def lmul(table, values):
    return jnp.tensordot(table, values, axes=1, precision=MATMUL_PRECISION)


def rmul(values, table):
    return jnp.tensordot(values, table, axes=1, precision=MATMUL_PRECISION)


def swap_leading(values):
    return lax.all_to_all(values, "seq", split_axis=0, concat_axis=0, tiled=True)


def rep_sum(*values):
    count = lax.axis_size("rep")
    if count & (count - 1):
        return lax.psum(values, "rep")
    dist = 1
    while dist < count:
        perm = [(i, i ^ dist) for i in range(count)]
        values = tuple(v + lax.ppermute(v, "rep", perm) for v in values)
        dist *= 2
    return values


def local_inverse(spec_re, spec_im, seq_count, slot_freq, offsets, modulus):
    rows_a = spec_re.shape[0]
    length_s = rows_a * LANES
    quota = spec_re.shape[2]
    sub = length_s // seq_count // LANES
    steps_a = jnp.arange(rows_a, dtype=jnp.int32)
    steps_b = jnp.arange(LANES, dtype=jnp.int32)
    last_re, last_im = unit_table(steps_b[:, None] * steps_b[None, :], LANES)
    u_re = rmul(spec_re, last_re) + rmul(spec_im, last_im)
    u_im = rmul(spec_im, last_re) - rmul(spec_re, last_im)
    tw_re, tw_im = unit_table(steps_a[:, None] * steps_b[None, :], length_s)
    tw_re = tw_re[:, None, None, :]
    tw_im = tw_im[:, None, None, :]
    u_re, u_im = (u_re * tw_re + u_im * tw_im, u_im * tw_re - u_re * tw_im)
    first_re, first_im = unit_table(steps_a[:, None] * steps_a[None, :], rows_a)
    out_re = lmul(first_re, u_re) + lmul(first_im, u_im)
    out_im = lmul(first_re, u_im) - lmul(first_im, u_re)
    dev = lax.axis_index("seq")
    is_first = dev == 0
    own_freq = (dev, jnp.where(is_first, seq_count, 2 * seq_count - dev))
    all_offsets = jnp.arange(length_s, dtype=jnp.int32)
    untwisted = []
    for p in range(2):
        twist_re, twist_im = unit_table(own_freq[p] * all_offsets, modulus)
        twist_re = twist_re.reshape(rows_a, 1, LANES)
        twist_im = twist_im.reshape(rows_a, 1, LANES)
        z_re = out_re[:, p]
        z_im = out_im[:, p]
        untwisted.append(
            (z_re * twist_re + z_im * twist_im, z_im * twist_re - z_re * twist_im)
        )
    send_a = untwisted[0][0]
    send_b = jnp.where(is_first, untwisted[1][0], untwisted[0][1])
    return (send_a, send_b)


def cross_inverse(send_a, send_b, seq_count):
    rows_a, quota = send_a.shape[:2]
    length_s = rows_a * LANES
    sub = length_s // seq_count // LANES
    both = jnp.stack([send_a, send_b], axis=0).reshape(2, seq_count, sub, quota, LANES)
    recv = swap_leading(both.transpose(1, 0, 3, 2, 4))
    sources = jnp.arange(seq_count, dtype=jnp.int32)
    mix_re, mix_im = unit_table(sources[:, None] * sources[None, :], 2 * seq_count)
    half_re, _ = unit_table(sources * seq_count, 2 * seq_count)
    first_src = (sources == 0)[None, :]
    mix = jnp.stack(
        [
            jnp.where(first_src, 1.0, 2.0 * mix_re),
            jnp.where(first_src, half_re[:, None], 2.0 * mix_im),
        ],
        axis=-1,
    ).reshape(seq_count, 2 * seq_count)
    rows_out = lmul(mix, recv.reshape(2 * seq_count, quota, sub, LANES))
    back = swap_leading(rows_out)
    return back.transpose(1, 0, 2, 3).reshape(quota, length_s)


def local(out_grad, gate_act, conv_out, value_act, filter_taps, skip_gain):
    batch_rows = out_grad.shape[0]
    channels = out_grad.shape[1]
    length_s = out_grad.shape[2]
    seq_count = lax.axis_size("seq")
    row_total = batch_rows * channels
    stack_rows = 2 * row_total + 1
    blk = length_s // seq_count
    sub = blk // LANES
    rows_a = length_s // LANES
    modulus = 2 * seq_count * length_s
    slot_freq = row_order(seq_count)
    offsets = lax.axis_index("seq") * blk + jnp.arange(blk, dtype=jnp.int32)

    gated_rows = out_grad.astype(jnp.float32) * gate_act.astype(jnp.float32)
    gate_grad = (out_grad.astype(jnp.float32) * conv_out.astype(jnp.float32)).astype(jnp.bfloat16)
    stacked = jnp.concatenate(
        [
            gated_rows.reshape(row_total, length_s),
            value_act.astype(jnp.float32).reshape(row_total, length_s),
            filter_taps.reshape(1, length_s),
        ],
        axis=0,
    )
    recv1 = swap_leading(
        stacked.reshape(stack_rows, seq_count, sub, LANES).transpose(1, 0, 2, 3)
    )
    sources = jnp.arange(seq_count, dtype=jnp.int32)
    cross_re, cross_im = unit_table(sources[:, None] * sources[None, :], 2 * seq_count)
    half_re, _ = unit_table(sources * seq_count, 2 * seq_count)
    cross = jnp.stack(
        [cross_re, jnp.where((sources == 0)[:, None], half_re[None, :], cross_im)], axis=1
    ).reshape(2 * seq_count, seq_count)
    mixed = lmul(cross, recv1).reshape(seq_count, 2, stack_rows, sub, LANES)
    recv2 = swap_leading(mixed)
    dev = lax.axis_index("seq")
    is_first = dev == 0
    own_freq = (dev, jnp.where(is_first, seq_count, 2 * seq_count - dev))
    keep_im = jnp.where(is_first, 0.0, 1.0)
    coef = (
        ((1.0, 0.0), (0.0, keep_im)),
        ((keep_im, 0.0), (1.0 - keep_im, -keep_im)),
    )
    steps_a = jnp.arange(rows_a, dtype=jnp.int32)
    steps_b = jnp.arange(LANES, dtype=jnp.int32)
    lane_step = modulus // LANES
    parts = []
    for p in range(2):
        phase = (steps_a[:, None] * steps_a[None, :]) % LANES * lane_step + (
            LANES * own_freq[p] * steps_a[None, :]
        )
        t_re, t_im = unit_table(phase, modulus)
        for c in range(2):
            cols = []
            for q in range(2):
                k_re, k_im = coef[p][q]
                if c == 0:
                    cols.append(t_re * k_re - t_im * k_im)
                else:
                    cols.append(t_re * k_im + t_im * k_re)
            parts.append(jnp.stack(cols, axis=-1))
    block = jnp.stack(parts, axis=1).reshape(4 * rows_a, seq_count, sub, 2)
    y1 = jnp.einsum(
        "mxyq,xqryl->mrl", block, recv2, precision=MATMUL_PRECISION
    )
    y1 = y1.reshape(rows_a, 2, 2, stack_rows, LANES)
    y2_re = []
    y2_im = []
    for p in range(2):
        phase = steps_b[None, :] * own_freq[p] + steps_a[:, None] * steps_b[None, :] * (
            2 * seq_count
        )
        tw_re, tw_im = unit_table(phase, modulus)
        tw_re = tw_re[:, None, :]
        tw_im = tw_im[:, None, :]
        y1_re = y1[:, p, 0]
        y1_im = y1[:, p, 1]
        y2_re.append(y1_re * tw_re - y1_im * tw_im)
        y2_im.append(y1_re * tw_im + y1_im * tw_re)
    y2_re = jnp.stack(y2_re, axis=1)
    y2_im = jnp.stack(y2_im, axis=1)
    last_re, last_im = unit_table(steps_b[:, None] * steps_b[None, :], LANES)
    spec_re = rmul(y2_re, last_re) - rmul(y2_im, last_im)
    spec_im = rmul(y2_re, last_im) + rmul(y2_im, last_re)
    grad_re = spec_re[:, :, :row_total]
    grad_im = spec_im[:, :, :row_total]
    value_re = spec_re[:, :, row_total : 2 * row_total]
    value_im = spec_im[:, :, row_total : 2 * row_total]
    filt_re = spec_re[:, :, 2 * row_total :]
    filt_im = spec_im[:, :, 2 * row_total :]
    carry_re = filt_re * grad_re + filt_im * grad_im
    carry_im = filt_re * grad_im - filt_im * grad_re
    lag_re = jnp.sum(grad_re * value_re + grad_im * value_im, axis=2, keepdims=True)
    lag_im = jnp.sum(grad_im * value_re - grad_re * value_im, axis=2, keepdims=True)
    rows_time = cross_inverse(
        *local_inverse(
            jnp.concatenate([carry_re, lag_re], axis=2),
            jnp.concatenate([carry_im, lag_im], axis=2),
            seq_count,
            slot_freq,
            offsets,
            modulus,
        ),
        seq_count,
    )
    (lag_time,) = rep_sum(rows_time[row_total:])
    rows_time = rows_time[:row_total]
    inv_points = 1.0 / modulus
    carried = (rows_time * inv_points).reshape(batch_rows, channels, length_s)
    value_grad = (carried + skip_gain[None, :, None] * gated_rows).astype(jnp.bfloat16)
    norm_scale = 1.0 / math.sqrt(
        batch_rows * lax.axis_size("rep") * channels * length_s * seq_count
    )
    filter_grad = lag_time[0] * inv_points * norm_scale
    return (gate_grad, value_grad, filter_grad)


def solution(mesh):
    return jax.shard_map(
        local,
        mesh=mesh,
        in_specs=(
            P("rep", None, "seq"),
            P("rep", None, "seq"),
            P("rep", None, "seq"),
            P("rep", None, "seq"),
            P("seq"),
            P(),
        ),
        out_specs=(P("rep", None, "seq"), P("rep", None, "seq"), P("seq")),
        check_vma=False,
    )
```

```python
import math

import jax
import jax.numpy as jnp
from jax import lax
from jax.sharding import PartitionSpec as P

MATMUL_PRECISION = lax.Precision.HIGH
LANES = 128


def unit_table(product, modulus):
    phase_rad = (product % modulus).astype(jnp.float32) * (-2.0 * math.pi / modulus)
    return (jnp.cos(phase_rad), jnp.sin(phase_rad))


def row_order(seq_count):
    slot_ids = jnp.arange(2 * seq_count, dtype=jnp.int32)
    owner_dev = slot_ids // 2
    second = jnp.where(owner_dev == 0, seq_count, 2 * seq_count - owner_dev)
    return jnp.where(slot_ids % 2 == 0, owner_dev, second)


def lmul(table, values):
    return jnp.tensordot(table, values, axes=1, precision=MATMUL_PRECISION)


def rmul(values, table):
    return jnp.tensordot(values, table, axes=1, precision=MATMUL_PRECISION)


def swap_leading(values):
    return lax.all_to_all(values, "seq", split_axis=0, concat_axis=0, tiled=True)


def rep_sum(*values):
    count = lax.axis_size("rep")
    if count & (count - 1):
        return lax.psum(values, "rep")
    dist = 1
    while dist < count:
        perm = [(i, i ^ dist) for i in range(count)]
        values = tuple(v + lax.ppermute(v, "rep", perm) for v in values)
        dist *= 2
    return values


def local_inverse(spec_re, spec_im, seq_count, slot_freq, offsets, modulus):
    rows_a = spec_re.shape[0]
    length_s = rows_a * LANES
    quota = spec_re.shape[2]
    sub = length_s // seq_count // LANES
    steps_a = jnp.arange(rows_a, dtype=jnp.int32)
    steps_b = jnp.arange(LANES, dtype=jnp.int32)
    last_re, last_im = unit_table(steps_b[:, None] * steps_b[None, :], LANES)
    u_re = rmul(spec_re, last_re) + rmul(spec_im, last_im)
    u_im = rmul(spec_im, last_re) - rmul(spec_re, last_im)
    tw_re, tw_im = unit_table(steps_a[:, None] * steps_b[None, :], length_s)
    tw_re = tw_re[:, None, None, :]
    tw_im = tw_im[:, None, None, :]
    u_re, u_im = (u_re * tw_re + u_im * tw_im, u_im * tw_re - u_re * tw_im)
    first_re, first_im = unit_table(steps_a[:, None] * steps_a[None, :], rows_a)
    out_re = lmul(first_re, u_re) + lmul(first_im, u_im)
    out_im = lmul(first_re, u_im) - lmul(first_im, u_re)
    dev = lax.axis_index("seq")
    is_first = dev == 0
    own_freq = (dev, jnp.where(is_first, seq_count, 2 * seq_count - dev))
    all_offsets = jnp.arange(length_s, dtype=jnp.int32)
    untwisted = []
    for p in range(2):
        twist_re, twist_im = unit_table(own_freq[p] * all_offsets, modulus)
        twist_re = twist_re.reshape(rows_a, 1, LANES)
        twist_im = twist_im.reshape(rows_a, 1, LANES)
        z_re = out_re[:, p]
        z_im = out_im[:, p]
        untwisted.append(
            (z_re * twist_re + z_im * twist_im, z_im * twist_re - z_re * twist_im)
        )
    send_a = untwisted[0][0]
    send_b = jnp.where(is_first, untwisted[1][0], untwisted[0][1])
    return (send_a, send_b)


def cross_inverse(send_a, send_b, seq_count):
    rows_a, quota = send_a.shape[:2]
    length_s = rows_a * LANES
    sub = length_s // seq_count // LANES
    both = jnp.stack([send_a, send_b], axis=0).reshape(2, seq_count, sub, quota, LANES)
    recv = swap_leading(both.transpose(1, 0, 3, 2, 4))
    sources = jnp.arange(seq_count, dtype=jnp.int32)
    mix_re, mix_im = unit_table(sources[:, None] * sources[None, :], 2 * seq_count)
    half_re, _ = unit_table(sources * seq_count, 2 * seq_count)
    first_src = (sources == 0)[None, :]
    mix = jnp.stack(
        [
            jnp.where(first_src, 1.0, 2.0 * mix_re),
            jnp.where(first_src, half_re[:, None], 2.0 * mix_im),
        ],
        axis=-1,
    ).reshape(seq_count, 2 * seq_count)
    rows_out = lmul(mix, recv.reshape(2 * seq_count, quota, sub, LANES))
    back = swap_leading(rows_out)
    return back.transpose(1, 0, 2, 3).reshape(quota, length_s)


def local(out_grad, gate_act, conv_out, value_act, filter_taps, skip_gain):
    batch_rows = out_grad.shape[0]
    channels = out_grad.shape[1]
    length_s = out_grad.shape[2]
    seq_count = lax.axis_size("seq")
    row_total = batch_rows * channels
    stack_rows = 2 * row_total + 1
    blk = length_s // seq_count
    sub = blk // LANES
    rows_a = length_s // LANES
    modulus = 2 * seq_count * length_s
    slot_freq = row_order(seq_count)
    offsets = lax.axis_index("seq") * blk + jnp.arange(blk, dtype=jnp.int32)

    gated_rows = out_grad.astype(jnp.float32) * gate_act.astype(jnp.float32)
    gate_grad = (out_grad.astype(jnp.float32) * conv_out.astype(jnp.float32)).astype(jnp.bfloat16)
    stacked = jnp.concatenate(
        [
            gated_rows.reshape(row_total, length_s),
            value_act.astype(jnp.float32).reshape(row_total, length_s),
            filter_taps.reshape(1, length_s),
        ],
        axis=0,
    )
    recv1 = swap_leading(
        stacked.reshape(stack_rows, seq_count, sub, LANES).transpose(1, 0, 2, 3)
    )
    sources = jnp.arange(seq_count, dtype=jnp.int32)
    cross_re, cross_im = unit_table(sources[:, None] * sources[None, :], 2 * seq_count)
    half_re, _ = unit_table(sources * seq_count, 2 * seq_count)
    cross = jnp.stack(
        [cross_re, jnp.where((sources == 0)[:, None], half_re[None, :], cross_im)], axis=1
    ).reshape(2 * seq_count, seq_count)
    mixed = lmul(cross, recv1).reshape(seq_count, 2, stack_rows, sub, LANES)
    recv2 = swap_leading(mixed.transpose(0, 3, 1, 2, 4))
    dev = lax.axis_index("seq")
    is_first = dev == 0
    own_freq = (dev, jnp.where(is_first, seq_count, 2 * seq_count - dev))
    keep_im = jnp.where(is_first, 0.0, 1.0)
    coef = (
        ((1.0, 0.0), (0.0, keep_im)),
        ((keep_im, 0.0), (1.0 - keep_im, -keep_im)),
    )
    steps_a = jnp.arange(rows_a, dtype=jnp.int32)
    steps_b = jnp.arange(LANES, dtype=jnp.int32)
    lane_step = modulus // LANES
    parts = []
    for p in range(2):
        phase = (steps_a[:, None] * steps_a[None, :]) % LANES * lane_step + (
            LANES * own_freq[p] * steps_a[None, :]
        )
        t_re, t_im = unit_table(phase, modulus)
        for c in range(2):
            cols = []
            for q in range(2):
                k_re, k_im = coef[p][q]
                if c == 0:
                    cols.append(t_re * k_re - t_im * k_im)
                else:
                    cols.append(t_re * k_im + t_im * k_re)
            parts.append(jnp.stack(cols, axis=-1))
    block = jnp.stack(parts, axis=1).reshape(4 * rows_a, 2 * rows_a)
    y1 = lmul(block, recv2.reshape(2 * rows_a, stack_rows * LANES))
    y1 = y1.reshape(rows_a, 2, 2, stack_rows, LANES)
    y2_re = []
    y2_im = []
    for p in range(2):
        phase = steps_b[None, :] * own_freq[p] + steps_a[:, None] * steps_b[None, :] * (
            2 * seq_count
        )
        tw_re, tw_im = unit_table(phase, modulus)
        tw_re = tw_re[:, None, :]
        tw_im = tw_im[:, None, :]
        y1_re = y1[:, p, 0]
        y1_im = y1[:, p, 1]
        y2_re.append(y1_re * tw_re - y1_im * tw_im)
        y2_im.append(y1_re * tw_im + y1_im * tw_re)
    y2_re = jnp.stack(y2_re, axis=1)
    y2_im = jnp.stack(y2_im, axis=1)
    last_re, last_im = unit_table(steps_b[:, None] * steps_b[None, :], LANES)
    spec_re = rmul(y2_re, last_re) - rmul(y2_im, last_im)
    spec_im = rmul(y2_re, last_im) + rmul(y2_im, last_re)
    grad_re = spec_re[:, :, :row_total]
    grad_im = spec_im[:, :, :row_total]
    value_re = spec_re[:, :, row_total : 2 * row_total]
    value_im = spec_im[:, :, row_total : 2 * row_total]
    filt_re = spec_re[:, :, 2 * row_total :]
    filt_im = spec_im[:, :, 2 * row_total :]
    carry_re = filt_re * grad_re + filt_im * grad_im
    carry_im = filt_re * grad_im - filt_im * grad_re
    lag_re = jnp.sum(grad_re * value_re + grad_im * value_im, axis=2, keepdims=True)
    lag_im = jnp.sum(grad_im * value_re - grad_re * value_im, axis=2, keepdims=True)
    rows_time = cross_inverse(
        *local_inverse(
            jnp.concatenate([carry_re, lag_re], axis=2),
            jnp.concatenate([carry_im, lag_im], axis=2),
            seq_count,
            slot_freq,
            offsets,
            modulus,
        ),
        seq_count,
    )
    (lag_time,) = rep_sum(rows_time[row_total:])
    rows_time = rows_time[:row_total]
    inv_points = 1.0 / modulus
    carried = (rows_time * inv_points).reshape(batch_rows, channels, length_s)
    value_grad = (carried + skip_gain[None, :, None] * gated_rows).astype(jnp.bfloat16)
    norm_scale = 1.0 / math.sqrt(
        batch_rows * lax.axis_size("rep") * channels * length_s * seq_count
    )
    filter_grad = lag_time[0] * inv_points * norm_scale
    return (gate_grad, value_grad, filter_grad)


def solution(mesh):
    return jax.shard_map(
        local,
        mesh=mesh,
        in_specs=(
            P("rep", None, "seq"),
            P("rep", None, "seq"),
            P("rep", None, "seq"),
            P("rep", None, "seq"),
            P("seq"),
            P(),
        ),
        out_specs=(P("rep", None, "seq"), P("rep", None, "seq"), P("seq")),
        check_vma=False,
    )
```

```python
import math

import jax
import jax.numpy as jnp
from jax import lax
from jax.sharding import PartitionSpec as P

MATMUL_PRECISION = lax.Precision.HIGH
LANES = 128


def unit_table(product, modulus):
    phase_rad = (product % modulus).astype(jnp.float32) * (-2.0 * math.pi / modulus)
    return (jnp.cos(phase_rad), jnp.sin(phase_rad))


def row_order(seq_count):
    slot_ids = jnp.arange(2 * seq_count, dtype=jnp.int32)
    owner_dev = slot_ids // 2
    second = jnp.where(owner_dev == 0, seq_count, 2 * seq_count - owner_dev)
    return jnp.where(slot_ids % 2 == 0, owner_dev, second)


def lmul(table, values):
    return jnp.tensordot(table, values, axes=1, precision=MATMUL_PRECISION)


def rmul(values, table):
    return jnp.tensordot(values, table, axes=1, precision=MATMUL_PRECISION)


def swap_leading(values):
    return lax.all_to_all(values, "seq", split_axis=0, concat_axis=0, tiled=True)


def rep_sum(*values):
    count = lax.axis_size("rep")
    me = lax.axis_index("rep")
    order = (me - jnp.arange(count, dtype=jnp.int32)) % count
    result = []
    for v in values:
        shifted = [v]
        for k in range(1, count):
            perm = [(i, (i + k) % count) for i in range(count)]
            shifted.append(lax.ppermute(v, "rep", perm))
        ordered = jnp.take(jnp.stack(shifted, axis=0), order, axis=0)
        total = ordered[0]
        for j in range(1, count):
            total = total + ordered[j]
        result.append(total)
    return tuple(result)


def local_inverse(spec_re, spec_im, seq_count, slot_freq, offsets, modulus):
    rows_a = spec_re.shape[0]
    length_s = rows_a * LANES
    quota = spec_re.shape[2]
    sub = length_s // seq_count // LANES
    steps_a = jnp.arange(rows_a, dtype=jnp.int32)
    steps_b = jnp.arange(LANES, dtype=jnp.int32)
    last_re, last_im = unit_table(steps_b[:, None] * steps_b[None, :], LANES)
    u_re = rmul(spec_re, last_re) + rmul(spec_im, last_im)
    u_im = rmul(spec_im, last_re) - rmul(spec_re, last_im)
    tw_re, tw_im = unit_table(steps_a[:, None] * steps_b[None, :], length_s)
    tw_re = tw_re[:, None, None, :]
    tw_im = tw_im[:, None, None, :]
    u_re, u_im = (u_re * tw_re + u_im * tw_im, u_im * tw_re - u_re * tw_im)
    first_re, first_im = unit_table(steps_a[:, None] * steps_a[None, :], rows_a)
    out_re = lmul(first_re, u_re) + lmul(first_im, u_im)
    out_im = lmul(first_re, u_im) - lmul(first_im, u_re)
    dev = lax.axis_index("seq")
    is_first = dev == 0
    own_freq = (dev, jnp.where(is_first, seq_count, 2 * seq_count - dev))
    all_offsets = jnp.arange(length_s, dtype=jnp.int32)
    untwisted = []
    for p in range(2):
        twist_re, twist_im = unit_table(own_freq[p] * all_offsets, modulus)
        twist_re = twist_re.reshape(rows_a, 1, LANES)
        twist_im = twist_im.reshape(rows_a, 1, LANES)
        z_re = out_re[:, p]
        z_im = out_im[:, p]
        untwisted.append(
            (z_re * twist_re + z_im * twist_im, z_im * twist_re - z_re * twist_im)
        )
    send_a = untwisted[0][0]
    send_b = jnp.where(is_first, untwisted[1][0], untwisted[0][1])
    return (send_a, send_b)


def cross_inverse(send_a, send_b, seq_count):
    rows_a, quota = send_a.shape[:2]
    length_s = rows_a * LANES
    sub = length_s // seq_count // LANES
    both = jnp.stack([send_a, send_b], axis=0).reshape(2, seq_count, sub, quota, LANES)
    recv = swap_leading(both.transpose(1, 0, 3, 2, 4))
    sources = jnp.arange(seq_count, dtype=jnp.int32)
    mix_re, mix_im = unit_table(sources[:, None] * sources[None, :], 2 * seq_count)
    half_re, _ = unit_table(sources * seq_count, 2 * seq_count)
    first_src = (sources == 0)[None, :]
    mix = jnp.stack(
        [
            jnp.where(first_src, 1.0, 2.0 * mix_re),
            jnp.where(first_src, half_re[:, None], 2.0 * mix_im),
        ],
        axis=-1,
    ).reshape(seq_count, 2 * seq_count)
    rows_out = lmul(mix, recv.reshape(2 * seq_count, quota, sub, LANES))
    back = swap_leading(rows_out)
    return back.transpose(1, 0, 2, 3).reshape(quota, length_s)


def local(out_grad, gate_act, conv_out, value_act, filter_taps, skip_gain):
    batch_rows = out_grad.shape[0]
    channels = out_grad.shape[1]
    length_s = out_grad.shape[2]
    seq_count = lax.axis_size("seq")
    row_total = batch_rows * channels
    stack_rows = 2 * row_total + 1
    blk = length_s // seq_count
    sub = blk // LANES
    rows_a = length_s // LANES
    modulus = 2 * seq_count * length_s
    slot_freq = row_order(seq_count)
    offsets = lax.axis_index("seq") * blk + jnp.arange(blk, dtype=jnp.int32)

    gated_rows = out_grad.astype(jnp.float32) * gate_act.astype(jnp.float32)
    gate_grad = (out_grad.astype(jnp.float32) * conv_out.astype(jnp.float32)).astype(jnp.bfloat16)
    stacked = jnp.concatenate(
        [
            gated_rows.reshape(row_total, length_s),
            value_act.astype(jnp.float32).reshape(row_total, length_s),
            filter_taps.reshape(1, length_s),
        ],
        axis=0,
    )
    recv1 = swap_leading(
        stacked.reshape(stack_rows, seq_count, sub, LANES).transpose(1, 0, 2, 3)
    )
    sources = jnp.arange(seq_count, dtype=jnp.int32)
    cross_re, cross_im = unit_table(sources[:, None] * sources[None, :], 2 * seq_count)
    half_re, _ = unit_table(sources * seq_count, 2 * seq_count)
    cross = jnp.stack(
        [cross_re, jnp.where((sources == 0)[:, None], half_re[None, :], cross_im)], axis=1
    ).reshape(2 * seq_count, seq_count)
    mixed = lmul(cross, recv1).reshape(seq_count, 2, stack_rows, sub, LANES)
    recv2 = swap_leading(mixed.transpose(0, 3, 1, 2, 4))
    dev = lax.axis_index("seq")
    is_first = dev == 0
    own_freq = (dev, jnp.where(is_first, seq_count, 2 * seq_count - dev))
    keep_im = jnp.where(is_first, 0.0, 1.0)
    coef = (
        ((1.0, 0.0), (0.0, keep_im)),
        ((keep_im, 0.0), (1.0 - keep_im, -keep_im)),
    )
    steps_a = jnp.arange(rows_a, dtype=jnp.int32)
    steps_b = jnp.arange(LANES, dtype=jnp.int32)
    lane_step = modulus // LANES
    parts = []
    for p in range(2):
        phase = (steps_a[:, None] * steps_a[None, :]) % LANES * lane_step + (
            LANES * own_freq[p] * steps_a[None, :]
        )
        t_re, t_im = unit_table(phase, modulus)
        for c in range(2):
            cols = []
            for q in range(2):
                k_re, k_im = coef[p][q]
                if c == 0:
                    cols.append(t_re * k_re - t_im * k_im)
                else:
                    cols.append(t_re * k_im + t_im * k_re)
            parts.append(jnp.stack(cols, axis=-1))
    block = jnp.stack(parts, axis=1).reshape(4 * rows_a, 2 * rows_a)
    y1 = lmul(block, recv2.reshape(2 * rows_a, stack_rows * LANES))
    y1 = y1.reshape(rows_a, 2, 2, stack_rows, LANES)
    y2_re = []
    y2_im = []
    for p in range(2):
        phase = steps_b[None, :] * own_freq[p] + steps_a[:, None] * steps_b[None, :] * (
            2 * seq_count
        )
        tw_re, tw_im = unit_table(phase, modulus)
        tw_re = tw_re[:, None, :]
        tw_im = tw_im[:, None, :]
        y1_re = y1[:, p, 0]
        y1_im = y1[:, p, 1]
        y2_re.append(y1_re * tw_re - y1_im * tw_im)
        y2_im.append(y1_re * tw_im + y1_im * tw_re)
    y2_re = jnp.stack(y2_re, axis=1)
    y2_im = jnp.stack(y2_im, axis=1)
    last_re, last_im = unit_table(steps_b[:, None] * steps_b[None, :], LANES)
    spec_re = rmul(y2_re, last_re) - rmul(y2_im, last_im)
    spec_im = rmul(y2_re, last_im) + rmul(y2_im, last_re)
    grad_re = spec_re[:, :, :row_total]
    grad_im = spec_im[:, :, :row_total]
    value_re = spec_re[:, :, row_total : 2 * row_total]
    value_im = spec_im[:, :, row_total : 2 * row_total]
    filt_re = spec_re[:, :, 2 * row_total :]
    filt_im = spec_im[:, :, 2 * row_total :]
    carry_re = filt_re * grad_re + filt_im * grad_im
    carry_im = filt_re * grad_im - filt_im * grad_re
    lag_re = jnp.sum(grad_re * value_re + grad_im * value_im, axis=2, keepdims=True)
    lag_im = jnp.sum(grad_im * value_re - grad_re * value_im, axis=2, keepdims=True)
    rows_time = cross_inverse(
        *local_inverse(
            jnp.concatenate([carry_re, lag_re], axis=2),
            jnp.concatenate([carry_im, lag_im], axis=2),
            seq_count,
            slot_freq,
            offsets,
            modulus,
        ),
        seq_count,
    )
    (lag_time,) = rep_sum(rows_time[row_total:])
    rows_time = rows_time[:row_total]
    inv_points = 1.0 / modulus
    carried = (rows_time * inv_points).reshape(batch_rows, channels, length_s)
    value_grad = (carried + skip_gain[None, :, None] * gated_rows).astype(jnp.bfloat16)
    norm_scale = 1.0 / math.sqrt(
        batch_rows * lax.axis_size("rep") * channels * length_s * seq_count
    )
    filter_grad = lag_time[0] * inv_points * norm_scale
    return (gate_grad, value_grad, filter_grad)


def solution(mesh):
    return jax.shard_map(
        local,
        mesh=mesh,
        in_specs=(
            P("rep", None, "seq"),
            P("rep", None, "seq"),
            P("rep", None, "seq"),
            P("rep", None, "seq"),
            P("seq"),
            P(),
        ),
        out_specs=(P("rep", None, "seq"), P("rep", None, "seq"), P("seq")),
        check_vma=False,
    )
```

```python
import math

import jax
import jax.numpy as jnp
from jax import lax
from jax.sharding import PartitionSpec as P

MATMUL_PRECISION = lax.Precision.HIGH
LANES = 128


def unit_table(product, modulus):
    phase_rad = (product % modulus).astype(jnp.float32) * (-2.0 * math.pi / modulus)
    return (jnp.cos(phase_rad), jnp.sin(phase_rad))


def row_order(seq_count):
    slot_ids = jnp.arange(2 * seq_count, dtype=jnp.int32)
    owner_dev = slot_ids // 2
    second = jnp.where(owner_dev == 0, seq_count, 2 * seq_count - owner_dev)
    return jnp.where(slot_ids % 2 == 0, owner_dev, second)


def lmul(table, values):
    return jnp.tensordot(table, values, axes=1, precision=MATMUL_PRECISION)


def rmul(values, table):
    return jnp.tensordot(values, table, axes=1, precision=MATMUL_PRECISION)


def swap_leading(values):
    return lax.all_to_all(values, "seq", split_axis=0, concat_axis=0, tiled=True)


def rep_sum(*values):
    count = lax.axis_size("rep")
    if count & (count - 1):
        return lax.psum(values, "rep")
    dist = 1
    while dist < count:
        perm = [(i, i ^ dist) for i in range(count)]
        values = tuple(v + lax.ppermute(v, "rep", perm) for v in values)
        dist *= 2
    return values


def local_inverse(spec_re, spec_im, seq_count, slot_freq, offsets, modulus):
    rows_a = spec_re.shape[0]
    length_s = rows_a * LANES
    quota = spec_re.shape[2]
    sub = length_s // seq_count // LANES
    steps_a = jnp.arange(rows_a, dtype=jnp.int32)
    steps_b = jnp.arange(LANES, dtype=jnp.int32)
    last_re, last_im = unit_table(steps_b[:, None] * steps_b[None, :], LANES)
    u_re = rmul(spec_re, last_re) + rmul(spec_im, last_im)
    u_im = rmul(spec_im, last_re) - rmul(spec_re, last_im)
    tw_re, tw_im = unit_table(steps_a[:, None] * steps_b[None, :], length_s)
    tw_re = tw_re[:, None, None, :]
    tw_im = tw_im[:, None, None, :]
    u_re, u_im = (u_re * tw_re + u_im * tw_im, u_im * tw_re - u_re * tw_im)
    first_re, first_im = unit_table(steps_a[:, None] * steps_a[None, :], rows_a)
    out_re = lmul(first_re, u_re) + lmul(first_im, u_im)
    out_im = lmul(first_re, u_im) - lmul(first_im, u_re)
    dev = lax.axis_index("seq")
    is_first = dev == 0
    own_freq = (dev, jnp.where(is_first, seq_count, 2 * seq_count - dev))
    all_offsets = jnp.arange(length_s, dtype=jnp.int32)
    untwisted = []
    for p in range(2):
        twist_re, twist_im = unit_table(own_freq[p] * all_offsets, modulus)
        twist_re = twist_re.reshape(rows_a, 1, LANES)
        twist_im = twist_im.reshape(rows_a, 1, LANES)
        z_re = out_re[:, p]
        z_im = out_im[:, p]
        untwisted.append(
            (z_re * twist_re + z_im * twist_im, z_im * twist_re - z_re * twist_im)
        )
    send_a = untwisted[0][0]
    send_b = jnp.where(is_first, untwisted[1][0], untwisted[0][1])
    return (send_a, send_b)


def cross_inverse(send_a, send_b, seq_count):
    rows_a, quota = send_a.shape[:2]
    length_s = rows_a * LANES
    sub = length_s // seq_count // LANES
    both = jnp.stack([send_a, send_b], axis=0).reshape(2, seq_count, sub, quota, LANES)
    recv = swap_leading(both.transpose(1, 0, 3, 2, 4))
    sources = jnp.arange(seq_count, dtype=jnp.int32)
    mix_re, mix_im = unit_table(sources[:, None] * sources[None, :], 2 * seq_count)
    half_re, _ = unit_table(sources * seq_count, 2 * seq_count)
    first_src = (sources == 0)[None, :]
    mix = jnp.stack(
        [
            jnp.where(first_src, 1.0, 2.0 * mix_re),
            jnp.where(first_src, half_re[:, None], 2.0 * mix_im),
        ],
        axis=-1,
    ).reshape(seq_count, 2 * seq_count)
    rows_out = lmul(mix, recv.reshape(2 * seq_count, quota, sub, LANES))
    back = swap_leading(rows_out)
    return back.transpose(1, 0, 2, 3).reshape(quota, length_s)


def local(out_grad, gate_act, conv_out, value_act, filter_taps, skip_gain):
    batch_rows = out_grad.shape[0]
    channels = out_grad.shape[1]
    length_s = out_grad.shape[2]
    seq_count = lax.axis_size("seq")
    row_total = batch_rows * channels
    stack_rows = 2 * row_total + 1
    blk = length_s // seq_count
    sub = blk // LANES
    rows_a = length_s // LANES
    modulus = 2 * seq_count * length_s
    slot_freq = row_order(seq_count)
    offsets = lax.axis_index("seq") * blk + jnp.arange(blk, dtype=jnp.int32)

    gated_rows = out_grad.astype(jnp.float32) * gate_act.astype(jnp.float32)
    gate_grad = (out_grad.astype(jnp.float32) * conv_out.astype(jnp.float32)).astype(jnp.bfloat16)
    stacked = jnp.concatenate(
        [
            gated_rows.reshape(row_total, length_s),
            value_act.astype(jnp.float32).reshape(row_total, length_s),
            filter_taps.reshape(1, length_s),
        ],
        axis=0,
    )
    recv1 = swap_leading(
        stacked.reshape(stack_rows, seq_count, sub, LANES).transpose(1, 0, 2, 3)
    )
    sources = jnp.arange(seq_count, dtype=jnp.int32)
    cross_re, cross_im = unit_table(sources[:, None] * sources[None, :], 2 * seq_count)
    half_re, _ = unit_table(sources * seq_count, 2 * seq_count)
    cross = jnp.stack(
        [cross_re, jnp.where((sources == 0)[:, None], half_re[None, :], cross_im)], axis=1
    ).reshape(2 * seq_count, seq_count)
    mixed = lmul(cross, recv1).reshape(seq_count, 2, stack_rows, sub, LANES)
    recv2 = swap_leading(mixed).transpose(0, 3, 1, 2, 4)
    dev = lax.axis_index("seq")
    is_first = dev == 0
    own_freq = (dev, jnp.where(is_first, seq_count, 2 * seq_count - dev))
    keep_im = jnp.where(is_first, 0.0, 1.0)
    coef = (
        ((1.0, 0.0), (0.0, keep_im)),
        ((keep_im, 0.0), (1.0 - keep_im, -keep_im)),
    )
    steps_a = jnp.arange(rows_a, dtype=jnp.int32)
    steps_b = jnp.arange(LANES, dtype=jnp.int32)
    lane_step = modulus // LANES
    parts = []
    for p in range(2):
        phase = (steps_a[:, None] * steps_a[None, :]) % LANES * lane_step + (
            LANES * own_freq[p] * steps_a[None, :]
        )
        t_re, t_im = unit_table(phase, modulus)
        for c in range(2):
            cols = []
            for q in range(2):
                k_re, k_im = coef[p][q]
                if c == 0:
                    cols.append(t_re * k_re - t_im * k_im)
                else:
                    cols.append(t_re * k_im + t_im * k_re)
            parts.append(jnp.stack(cols, axis=-1))
    block = jnp.stack(parts, axis=1).reshape(4 * rows_a, 2 * rows_a)
    y1 = lmul(block, recv2.reshape(2 * rows_a, stack_rows * LANES))
    y1 = y1.reshape(rows_a, 2, 2, stack_rows, LANES)
    y2_re = []
    y2_im = []
    for p in range(2):
        phase = steps_b[None, :] * own_freq[p] + steps_a[:, None] * steps_b[None, :] * (
            2 * seq_count
        )
        tw_re, tw_im = unit_table(phase, modulus)
        tw_re = tw_re[:, None, :]
        tw_im = tw_im[:, None, :]
        y1_re = y1[:, p, 0]
        y1_im = y1[:, p, 1]
        y2_re.append(y1_re * tw_re - y1_im * tw_im)
        y2_im.append(y1_re * tw_im + y1_im * tw_re)
    y2_re = jnp.stack(y2_re, axis=1)
    y2_im = jnp.stack(y2_im, axis=1)
    last_re, last_im = unit_table(steps_b[:, None] * steps_b[None, :], LANES)
    spec_re = rmul(y2_re, last_re) - rmul(y2_im, last_im)
    spec_im = rmul(y2_re, last_im) + rmul(y2_im, last_re)
    grad_re = spec_re[:, :, :row_total]
    grad_im = spec_im[:, :, :row_total]
    value_re = spec_re[:, :, row_total : 2 * row_total]
    value_im = spec_im[:, :, row_total : 2 * row_total]
    filt_re = spec_re[:, :, 2 * row_total :]
    filt_im = spec_im[:, :, 2 * row_total :]
    carry_re = filt_re * grad_re + filt_im * grad_im
    carry_im = filt_re * grad_im - filt_im * grad_re
    lag_re = jnp.sum(grad_re * value_re + grad_im * value_im, axis=2, keepdims=True)
    lag_im = jnp.sum(grad_im * value_re - grad_re * value_im, axis=2, keepdims=True)
    rows_time = cross_inverse(
        *local_inverse(
            jnp.concatenate([carry_re, lag_re], axis=2),
            jnp.concatenate([carry_im, lag_im], axis=2),
            seq_count,
            slot_freq,
            offsets,
            modulus,
        ),
        seq_count,
    )
    (lag_time,) = rep_sum(rows_time[row_total:])
    rows_time = rows_time[:row_total]
    inv_points = 1.0 / modulus
    carried = (rows_time * inv_points).reshape(batch_rows, channels, length_s)
    value_grad = (carried + skip_gain[None, :, None] * gated_rows).astype(jnp.bfloat16)
    norm_scale = 1.0 / math.sqrt(
        batch_rows * lax.axis_size("rep") * channels * length_s * seq_count
    )
    filter_grad = lag_time[0] * inv_points * norm_scale
    return (gate_grad, value_grad, filter_grad)


def solution(mesh):
    return jax.shard_map(
        local,
        mesh=mesh,
        in_specs=(
            P("rep", None, "seq"),
            P("rep", None, "seq"),
            P("rep", None, "seq"),
            P("rep", None, "seq"),
            P("seq"),
            P(),
        ),
        out_specs=(P("rep", None, "seq"), P("rep", None, "seq"), P("seq")),
        check_vma=False,
    )
```

```python
import math

import jax
import jax.numpy as jnp
from jax import lax
from jax.sharding import PartitionSpec as P

MATMUL_PRECISION = lax.Precision.HIGH
LANES = 128


def unit_table(product, modulus):
    phase_rad = (product % modulus).astype(jnp.float32) * (-2.0 * math.pi / modulus)
    return (jnp.cos(phase_rad), jnp.sin(phase_rad))


def row_order(seq_count):
    slot_ids = jnp.arange(2 * seq_count, dtype=jnp.int32)
    owner_dev = slot_ids // 2
    second = jnp.where(owner_dev == 0, seq_count, 2 * seq_count - owner_dev)
    return jnp.where(slot_ids % 2 == 0, owner_dev, second)


def lmul(table, values):
    return jnp.tensordot(table, values, axes=1, precision=MATMUL_PRECISION)


def rmul(values, table):
    return jnp.tensordot(values, table, axes=1, precision=MATMUL_PRECISION)


def swap_leading(values):
    return lax.all_to_all(values, "seq", split_axis=0, concat_axis=0, tiled=True)


def rep_sum(*values):
    count = lax.axis_size("rep")
    if count & (count - 1):
        return lax.psum(values, "rep")
    dist = 1
    while dist < count:
        perm = [(i, i ^ dist) for i in range(count)]
        values = tuple(v + lax.ppermute(v, "rep", perm) for v in values)
        dist *= 2
    return values


def local_inverse(spec_re, spec_im, seq_count, slot_freq, offsets, modulus):
    rows_a = spec_re.shape[0]
    length_s = rows_a * LANES
    quota = spec_re.shape[2]
    sub = length_s // seq_count // LANES
    steps_a = jnp.arange(rows_a, dtype=jnp.int32)
    steps_b = jnp.arange(LANES, dtype=jnp.int32)
    last_re, last_im = unit_table(steps_b[:, None] * steps_b[None, :], LANES)
    u_re = rmul(spec_re, last_re) + rmul(spec_im, last_im)
    u_im = rmul(spec_im, last_re) - rmul(spec_re, last_im)
    tw_re, tw_im = unit_table(steps_a[:, None] * steps_b[None, :], length_s)
    tw_re = tw_re[:, None, None, :]
    tw_im = tw_im[:, None, None, :]
    u_re, u_im = (u_re * tw_re + u_im * tw_im, u_im * tw_re - u_re * tw_im)
    first_re, first_im = unit_table(steps_a[:, None] * steps_a[None, :], rows_a)
    out_re = lmul(first_re, u_re) + lmul(first_im, u_im)
    out_im = lmul(first_re, u_im) - lmul(first_im, u_re)
    dev = lax.axis_index("seq")
    is_first = dev == 0
    own_freq = (dev, jnp.where(is_first, seq_count, 2 * seq_count - dev))
    all_offsets = jnp.arange(length_s, dtype=jnp.int32)
    untwisted = []
    for p in range(2):
        twist_re, twist_im = unit_table(own_freq[p] * all_offsets, modulus)
        twist_re = twist_re.reshape(rows_a, 1, LANES)
        twist_im = twist_im.reshape(rows_a, 1, LANES)
        z_re = out_re[:, p]
        z_im = out_im[:, p]
        untwisted.append(
            (z_re * twist_re + z_im * twist_im, z_im * twist_re - z_re * twist_im)
        )
    send_a = untwisted[0][0]
    send_b = jnp.where(is_first, untwisted[1][0], untwisted[0][1])
    return (send_a, send_b)


def cross_inverse(send_a, send_b, seq_count):
    rows_a, quota = send_a.shape[:2]
    length_s = rows_a * LANES
    sub = length_s // seq_count // LANES
    both = jnp.stack([send_a, send_b], axis=0).reshape(2, seq_count, sub, quota, LANES)
    recv = swap_leading(both.transpose(1, 0, 3, 2, 4))
    sources = jnp.arange(seq_count, dtype=jnp.int32)
    mix_re, mix_im = unit_table(sources[:, None] * sources[None, :], 2 * seq_count)
    half_re, _ = unit_table(sources * seq_count, 2 * seq_count)
    first_src = (sources == 0)[None, :]
    mix = jnp.stack(
        [
            jnp.where(first_src, 1.0, 2.0 * mix_re),
            jnp.where(first_src, half_re[:, None], 2.0 * mix_im),
        ],
        axis=-1,
    ).reshape(seq_count, 2 * seq_count)
    rows_out = lmul(mix, recv.reshape(2 * seq_count, quota, sub, LANES))
    back = swap_leading(rows_out)
    return back.transpose(1, 0, 2, 3).reshape(quota, length_s)


def local(out_grad, gate_act, conv_out, value_act, filter_taps, skip_gain):
    batch_rows = out_grad.shape[0]
    channels = out_grad.shape[1]
    length_s = out_grad.shape[2]
    seq_count = lax.axis_size("seq")
    row_total = batch_rows * channels
    stack_rows = 2 * row_total + 1
    blk = length_s // seq_count
    sub = blk // LANES
    rows_a = length_s // LANES
    modulus = 2 * seq_count * length_s
    slot_freq = row_order(seq_count)
    offsets = lax.axis_index("seq") * blk + jnp.arange(blk, dtype=jnp.int32)

    gated_rows = out_grad.astype(jnp.float32) * gate_act.astype(jnp.float32)
    gate_grad = (out_grad.astype(jnp.float32) * conv_out.astype(jnp.float32)).astype(jnp.bfloat16)
    stacked = jnp.concatenate(
        [
            gated_rows.reshape(row_total, length_s),
            filter_taps.reshape(1, length_s),
            value_act.astype(jnp.float32).reshape(row_total, length_s),
        ],
        axis=0,
    )
    recv1 = swap_leading(
        stacked.reshape(stack_rows, seq_count, sub, LANES).transpose(1, 0, 2, 3)
    )
    sources = jnp.arange(seq_count, dtype=jnp.int32)
    cross_re, cross_im = unit_table(sources[:, None] * sources[None, :], 2 * seq_count)
    half_re, _ = unit_table(sources * seq_count, 2 * seq_count)
    cross = jnp.stack(
        [cross_re, jnp.where((sources == 0)[:, None], half_re[None, :], cross_im)], axis=1
    ).reshape(2 * seq_count, seq_count)
    mixed = lmul(cross, recv1).reshape(seq_count, 2, stack_rows, sub, LANES)
    dev = lax.axis_index("seq")
    is_first = dev == 0
    own_freq = (dev, jnp.where(is_first, seq_count, 2 * seq_count - dev))
    keep_im = jnp.where(is_first, 0.0, 1.0)
    coef = (
        ((1.0, 0.0), (0.0, keep_im)),
        ((keep_im, 0.0), (1.0 - keep_im, -keep_im)),
    )
    steps_a = jnp.arange(rows_a, dtype=jnp.int32)
    steps_b = jnp.arange(LANES, dtype=jnp.int32)
    lane_step = modulus // LANES
    parts = []
    for p in range(2):
        phase = (steps_a[:, None] * steps_a[None, :]) % LANES * lane_step + (
            LANES * own_freq[p] * steps_a[None, :]
        )
        t_re, t_im = unit_table(phase, modulus)
        for c in range(2):
            cols = []
            for q in range(2):
                k_re, k_im = coef[p][q]
                if c == 0:
                    cols.append(t_re * k_re - t_im * k_im)
                else:
                    cols.append(t_re * k_im + t_im * k_re)
            parts.append(jnp.stack(cols, axis=-1))
    block = jnp.stack(parts, axis=1).reshape(4 * rows_a, 2 * rows_a)
    specs = []
    for lo, hi in ((0, row_total + 1), (row_total + 1, stack_rows)):
        part_rows = hi - lo
        recv2 = swap_leading(mixed[:, :, lo:hi]).transpose(0, 3, 1, 2, 4)
        y1 = lmul(block, recv2.reshape(2 * rows_a, part_rows * LANES))
        y1 = y1.reshape(rows_a, 2, 2, part_rows, LANES)
        y2_re = []
        y2_im = []
        for p in range(2):
            phase = steps_b[None, :] * own_freq[p] + steps_a[:, None] * steps_b[None, :] * (
                2 * seq_count
            )
            tw_re, tw_im = unit_table(phase, modulus)
            tw_re = tw_re[:, None, :]
            tw_im = tw_im[:, None, :]
            y1_re = y1[:, p, 0]
            y1_im = y1[:, p, 1]
            y2_re.append(y1_re * tw_re - y1_im * tw_im)
            y2_im.append(y1_re * tw_im + y1_im * tw_re)
        y2_re = jnp.stack(y2_re, axis=1)
        y2_im = jnp.stack(y2_im, axis=1)
        last_re, last_im = unit_table(steps_b[:, None] * steps_b[None, :], LANES)
        spec_re = rmul(y2_re, last_re) - rmul(y2_im, last_im)
        spec_im = rmul(y2_re, last_im) + rmul(y2_im, last_re)
        specs.append((spec_re, spec_im))
    grad_re = specs[0][0][:, :, :row_total]
    grad_im = specs[0][1][:, :, :row_total]
    filt_re = specs[0][0][:, :, row_total:]
    filt_im = specs[0][1][:, :, row_total:]
    value_re, value_im = specs[1]
    carry_re = filt_re * grad_re + filt_im * grad_im
    carry_im = filt_re * grad_im - filt_im * grad_re
    carry_a, carry_b = local_inverse(carry_re, carry_im, seq_count, slot_freq, offsets, modulus)
    lag_re = jnp.sum(grad_re * value_re + grad_im * value_im, axis=2, keepdims=True)
    lag_im = jnp.sum(grad_im * value_re - grad_re * value_im, axis=2, keepdims=True)
    lag_a, lag_b = local_inverse(lag_re, lag_im, seq_count, slot_freq, offsets, modulus)
    rows_time = cross_inverse(
        jnp.concatenate([carry_a, lag_a], axis=1),
        jnp.concatenate([carry_b, lag_b], axis=1),
        seq_count,
    )
    (lag_time,) = rep_sum(rows_time[row_total:])
    rows_time = rows_time[:row_total]
    inv_points = 1.0 / modulus
    carried = (rows_time * inv_points).reshape(batch_rows, channels, length_s)
    value_grad = (carried + skip_gain[None, :, None] * gated_rows).astype(jnp.bfloat16)
    norm_scale = 1.0 / math.sqrt(
        batch_rows * lax.axis_size("rep") * channels * length_s * seq_count
    )
    filter_grad = lag_time[0] * inv_points * norm_scale
    return (gate_grad, value_grad, filter_grad)


def solution(mesh):
    return jax.shard_map(
        local,
        mesh=mesh,
        in_specs=(
            P("rep", None, "seq"),
            P("rep", None, "seq"),
            P("rep", None, "seq"),
            P("rep", None, "seq"),
            P("seq"),
            P(),
        ),
        out_specs=(P("rep", None, "seq"), P("rep", None, "seq"), P("seq")),
        check_vma=False,
    )
```

```python
import math

import jax
import jax.numpy as jnp
from jax import lax
from jax.sharding import PartitionSpec as P

MATMUL_PRECISION = lax.Precision.HIGH
LANES = 128


def unit_table(product, modulus):
    phase_rad = (product % modulus).astype(jnp.float32) * (-2.0 * math.pi / modulus)
    return (jnp.cos(phase_rad), jnp.sin(phase_rad))


def row_order(seq_count):
    slot_ids = jnp.arange(2 * seq_count, dtype=jnp.int32)
    owner_dev = slot_ids // 2
    second = jnp.where(owner_dev == 0, seq_count, 2 * seq_count - owner_dev)
    return jnp.where(slot_ids % 2 == 0, owner_dev, second)


def lmul(table, values):
    return jnp.tensordot(table, values, axes=1, precision=MATMUL_PRECISION)


def rmul(values, table):
    return jnp.tensordot(values, table, axes=1, precision=MATMUL_PRECISION)


def swap_leading(values):
    return lax.all_to_all(values, "seq", split_axis=0, concat_axis=0, tiled=True)


def rep_sum(*values):
    count = lax.axis_size("rep")
    if count & (count - 1):
        return lax.psum(values, "rep")
    dist = 1
    while dist < count:
        perm = [(i, i ^ dist) for i in range(count)]
        values = tuple(v + lax.ppermute(v, "rep", perm) for v in values)
        dist *= 2
    return values


def local_inverse(spec_re, spec_im, seq_count, slot_freq, offsets, modulus):
    rows_a = spec_re.shape[0]
    length_s = rows_a * LANES
    quota = spec_re.shape[2]
    sub = length_s // seq_count // LANES
    steps_a = jnp.arange(rows_a, dtype=jnp.int32)
    steps_b = jnp.arange(LANES, dtype=jnp.int32)
    last_re, last_im = unit_table(steps_b[:, None] * steps_b[None, :], LANES)
    u_re = rmul(spec_re, last_re) + rmul(spec_im, last_im)
    u_im = rmul(spec_im, last_re) - rmul(spec_re, last_im)
    tw_re, tw_im = unit_table(steps_a[:, None] * steps_b[None, :], length_s)
    tw_re = tw_re[:, None, None, :]
    tw_im = tw_im[:, None, None, :]
    u_re, u_im = (u_re * tw_re + u_im * tw_im, u_im * tw_re - u_re * tw_im)
    first_re, first_im = unit_table(steps_a[:, None] * steps_a[None, :], rows_a)
    out_re = lmul(first_re, u_re) + lmul(first_im, u_im)
    out_im = lmul(first_re, u_im) - lmul(first_im, u_re)
    dev = lax.axis_index("seq")
    is_first = dev == 0
    own_freq = (dev, jnp.where(is_first, seq_count, 2 * seq_count - dev))
    all_offsets = jnp.arange(length_s, dtype=jnp.int32)
    untwisted = []
    for p in range(2):
        twist_re, twist_im = unit_table(own_freq[p] * all_offsets, modulus)
        twist_re = twist_re.reshape(rows_a, 1, LANES)
        twist_im = twist_im.reshape(rows_a, 1, LANES)
        z_re = out_re[:, p]
        z_im = out_im[:, p]
        untwisted.append(
            (z_re * twist_re + z_im * twist_im, z_im * twist_re - z_re * twist_im)
        )
    send_a = untwisted[0][0]
    send_b = jnp.where(is_first, untwisted[1][0], untwisted[0][1])
    return (send_a, send_b)


def cross_inverse(send_a, send_b, seq_count):
    rows_a, quota = send_a.shape[:2]
    length_s = rows_a * LANES
    sub = length_s // seq_count // LANES
    both = jnp.stack([send_a, send_b], axis=0).reshape(2, seq_count, sub, quota, LANES)
    recv = swap_leading(both.transpose(1, 0, 3, 2, 4))
    sources = jnp.arange(seq_count, dtype=jnp.int32)
    mix_re, mix_im = unit_table(sources[:, None] * sources[None, :], 2 * seq_count)
    half_re, _ = unit_table(sources * seq_count, 2 * seq_count)
    first_src = (sources == 0)[None, :]
    mix = jnp.stack(
        [
            jnp.where(first_src, 1.0, 2.0 * mix_re),
            jnp.where(first_src, half_re[:, None], 2.0 * mix_im),
        ],
        axis=-1,
    ).reshape(seq_count, 2 * seq_count)
    rows_out = lmul(mix, recv.reshape(2 * seq_count, quota, sub, LANES))
    back = swap_leading(rows_out)
    return back.transpose(1, 0, 2, 3).reshape(quota, length_s)


def local(out_grad, gate_act, conv_out, value_act, filter_taps, skip_gain):
    batch_rows = out_grad.shape[0]
    channels = out_grad.shape[1]
    length_s = out_grad.shape[2]
    seq_count = lax.axis_size("seq")
    row_total = batch_rows * channels
    stack_rows = 2 * row_total + 1
    blk = length_s // seq_count
    sub = blk // LANES
    rows_a = length_s // LANES
    modulus = 2 * seq_count * length_s
    slot_freq = row_order(seq_count)
    offsets = lax.axis_index("seq") * blk + jnp.arange(blk, dtype=jnp.int32)

    gated_rows = out_grad.astype(jnp.float32) * gate_act.astype(jnp.float32)
    gate_grad = (out_grad.astype(jnp.float32) * conv_out.astype(jnp.float32)).astype(jnp.bfloat16)
    stacked = jnp.concatenate(
        [
            gated_rows.reshape(row_total, length_s),
            value_act.astype(jnp.float32).reshape(row_total, length_s),
            filter_taps.reshape(1, length_s),
        ],
        axis=0,
    )
    recv1 = swap_leading(
        stacked.reshape(stack_rows, seq_count, sub, LANES).transpose(1, 0, 2, 3)
    )
    sources = jnp.arange(seq_count, dtype=jnp.int32)
    cross_re, cross_im = unit_table(sources[:, None] * sources[None, :], 2 * seq_count)
    half_re, _ = unit_table(sources * seq_count, 2 * seq_count)
    cross = jnp.stack(
        [cross_re, jnp.where((sources == 0)[:, None], half_re[None, :], cross_im)], axis=1
    ).reshape(2 * seq_count, seq_count)
    mixed = lmul(cross, recv1).reshape(seq_count, 2, stack_rows, sub, LANES)
    padded_rows = -(-stack_rows // 8) * 8
    recv2 = swap_leading(
        jnp.pad(
            mixed.transpose(0, 3, 1, 2, 4),
            ((0, 0), (0, 0), (0, 0), (0, padded_rows - stack_rows), (0, 0)),
        )
    )
    dev = lax.axis_index("seq")
    is_first = dev == 0
    own_freq = (dev, jnp.where(is_first, seq_count, 2 * seq_count - dev))
    keep_im = jnp.where(is_first, 0.0, 1.0)
    coef = (
        ((1.0, 0.0), (0.0, keep_im)),
        ((keep_im, 0.0), (1.0 - keep_im, -keep_im)),
    )
    steps_a = jnp.arange(rows_a, dtype=jnp.int32)
    steps_b = jnp.arange(LANES, dtype=jnp.int32)
    lane_step = modulus // LANES
    parts = []
    for p in range(2):
        phase = (steps_a[:, None] * steps_a[None, :]) % LANES * lane_step + (
            LANES * own_freq[p] * steps_a[None, :]
        )
        t_re, t_im = unit_table(phase, modulus)
        for c in range(2):
            cols = []
            for q in range(2):
                k_re, k_im = coef[p][q]
                if c == 0:
                    cols.append(t_re * k_re - t_im * k_im)
                else:
                    cols.append(t_re * k_im + t_im * k_re)
            parts.append(jnp.stack(cols, axis=-1))
    block = jnp.stack(parts, axis=1).reshape(4 * rows_a, 2 * rows_a)
    y1 = lmul(block, recv2.reshape(2 * rows_a, padded_rows * LANES))
    y1 = y1.reshape(rows_a, 2, 2, padded_rows, LANES)[:, :, :, :stack_rows]
    y2_re = []
    y2_im = []
    for p in range(2):
        phase = steps_b[None, :] * own_freq[p] + steps_a[:, None] * steps_b[None, :] * (
            2 * seq_count
        )
        tw_re, tw_im = unit_table(phase, modulus)
        tw_re = tw_re[:, None, :]
        tw_im = tw_im[:, None, :]
        y1_re = y1[:, p, 0]
        y1_im = y1[:, p, 1]
        y2_re.append(y1_re * tw_re - y1_im * tw_im)
        y2_im.append(y1_re * tw_im + y1_im * tw_re)
    y2_re = jnp.stack(y2_re, axis=1)
    y2_im = jnp.stack(y2_im, axis=1)
    last_re, last_im = unit_table(steps_b[:, None] * steps_b[None, :], LANES)
    spec_re = rmul(y2_re, last_re) - rmul(y2_im, last_im)
    spec_im = rmul(y2_re, last_im) + rmul(y2_im, last_re)
    grad_re = spec_re[:, :, :row_total]
    grad_im = spec_im[:, :, :row_total]
    value_re = spec_re[:, :, row_total : 2 * row_total]
    value_im = spec_im[:, :, row_total : 2 * row_total]
    filt_re = spec_re[:, :, 2 * row_total :]
    filt_im = spec_im[:, :, 2 * row_total :]
    carry_re = filt_re * grad_re + filt_im * grad_im
    carry_im = filt_re * grad_im - filt_im * grad_re
    lag_re = jnp.sum(grad_re * value_re + grad_im * value_im, axis=2, keepdims=True)
    lag_im = jnp.sum(grad_im * value_re - grad_re * value_im, axis=2, keepdims=True)
    rows_time = cross_inverse(
        *local_inverse(
            jnp.concatenate([carry_re, lag_re], axis=2),
            jnp.concatenate([carry_im, lag_im], axis=2),
            seq_count,
            slot_freq,
            offsets,
            modulus,
        ),
        seq_count,
    )
    (lag_time,) = rep_sum(rows_time[row_total:])
    rows_time = rows_time[:row_total]
    inv_points = 1.0 / modulus
    carried = (rows_time * inv_points).reshape(batch_rows, channels, length_s)
    value_grad = (carried + skip_gain[None, :, None] * gated_rows).astype(jnp.bfloat16)
    norm_scale = 1.0 / math.sqrt(
        batch_rows * lax.axis_size("rep") * channels * length_s * seq_count
    )
    filter_grad = lag_time[0] * inv_points * norm_scale
    return (gate_grad, value_grad, filter_grad)


def solution(mesh):
    return jax.shard_map(
        local,
        mesh=mesh,
        in_specs=(
            P("rep", None, "seq"),
            P("rep", None, "seq"),
            P("rep", None, "seq"),
            P("rep", None, "seq"),
            P("seq"),
            P(),
        ),
        out_specs=(P("rep", None, "seq"), P("rep", None, "seq"), P("seq")),
        check_vma=False,
    )
```

```python
import math

import jax
import jax.numpy as jnp
from jax import lax
from jax.sharding import PartitionSpec as P

MATMUL_PRECISION = lax.Precision.HIGH
LANES = 128


def unit_table(product, modulus):
    phase_rad = (product % modulus).astype(jnp.float32) * (-2.0 * math.pi / modulus)
    return (jnp.cos(phase_rad), jnp.sin(phase_rad))


def row_order(seq_count):
    slot_ids = jnp.arange(2 * seq_count, dtype=jnp.int32)
    owner_dev = slot_ids // 2
    second = jnp.where(owner_dev == 0, seq_count, 2 * seq_count - owner_dev)
    return jnp.where(slot_ids % 2 == 0, owner_dev, second)


def lmul(table, values):
    return jnp.tensordot(table, values, axes=1, precision=MATMUL_PRECISION)


def rmul(values, table):
    return jnp.tensordot(values, table, axes=1, precision=MATMUL_PRECISION)


def swap_leading(values):
    return lax.all_to_all(values, "seq", split_axis=0, concat_axis=0, tiled=True)


def rep_sum(*values):
    count = lax.axis_size("rep")
    if count & (count - 1):
        return lax.psum(values, "rep")
    dist = 1
    while dist < count:
        perm = [(i, i ^ dist) for i in range(count)]
        values = tuple(v + lax.ppermute(v, "rep", perm) for v in values)
        dist *= 2
    return values


def local_inverse(spec_re, spec_im, seq_count, slot_freq, offsets, modulus):
    rows_a = spec_re.shape[0]
    length_s = rows_a * LANES
    quota = spec_re.shape[2]
    sub = length_s // seq_count // LANES
    steps_a = jnp.arange(rows_a, dtype=jnp.int32)
    steps_b = jnp.arange(LANES, dtype=jnp.int32)
    last_re, last_im = unit_table(steps_b[:, None] * steps_b[None, :], LANES)
    u_re = rmul(spec_re, last_re) + rmul(spec_im, last_im)
    u_im = rmul(spec_im, last_re) - rmul(spec_re, last_im)
    tw_re, tw_im = unit_table(steps_a[:, None] * steps_b[None, :], length_s)
    tw_re = tw_re[:, None, None, :]
    tw_im = tw_im[:, None, None, :]
    u_re, u_im = (u_re * tw_re + u_im * tw_im, u_im * tw_re - u_re * tw_im)
    first_re, first_im = unit_table(steps_a[:, None] * steps_a[None, :], rows_a)
    out_re = lmul(first_re, u_re) + lmul(first_im, u_im)
    out_im = lmul(first_re, u_im) - lmul(first_im, u_re)
    dev = lax.axis_index("seq")
    is_first = dev == 0
    own_freq = (dev, jnp.where(is_first, seq_count, 2 * seq_count - dev))
    all_offsets = jnp.arange(length_s, dtype=jnp.int32)
    untwisted = []
    for p in range(2):
        twist_re, twist_im = unit_table(own_freq[p] * all_offsets, modulus)
        twist_re = twist_re.reshape(rows_a, 1, LANES)
        twist_im = twist_im.reshape(rows_a, 1, LANES)
        z_re = out_re[:, p]
        z_im = out_im[:, p]
        untwisted.append(
            (z_re * twist_re + z_im * twist_im, z_im * twist_re - z_re * twist_im)
        )
    send_a = untwisted[0][0]
    send_b = jnp.where(is_first, untwisted[1][0], untwisted[0][1])
    return (send_a, send_b)


def cross_inverse(send_a, send_b, seq_count):
    rows_a, quota = send_a.shape[:2]
    length_s = rows_a * LANES
    sub = length_s // seq_count // LANES
    both = jnp.stack([send_a, send_b], axis=0).reshape(2, seq_count, sub, quota, LANES)
    recv = swap_leading(both.transpose(1, 0, 3, 2, 4))
    sources = jnp.arange(seq_count, dtype=jnp.int32)
    mix_re, mix_im = unit_table(sources[:, None] * sources[None, :], 2 * seq_count)
    half_re, _ = unit_table(sources * seq_count, 2 * seq_count)
    first_src = (sources == 0)[None, :]
    mix = jnp.stack(
        [
            jnp.where(first_src, 1.0, 2.0 * mix_re),
            jnp.where(first_src, half_re[:, None], 2.0 * mix_im),
        ],
        axis=-1,
    ).reshape(seq_count, 2 * seq_count)
    rows_out = lmul(mix, recv.reshape(2 * seq_count, quota, sub, LANES))
    (lag_out,) = rep_sum(rows_out[:, quota - 1 :])
    back = swap_leading(rows_out[:, : quota - 1])
    lag_back = swap_leading(lag_out)
    return (
        back.transpose(1, 0, 2, 3).reshape(quota - 1, length_s),
        lag_back.transpose(1, 0, 2, 3).reshape(1, length_s),
    )


def local(out_grad, gate_act, conv_out, value_act, filter_taps, skip_gain):
    batch_rows = out_grad.shape[0]
    channels = out_grad.shape[1]
    length_s = out_grad.shape[2]
    seq_count = lax.axis_size("seq")
    row_total = batch_rows * channels
    stack_rows = 2 * row_total + 1
    blk = length_s // seq_count
    sub = blk // LANES
    rows_a = length_s // LANES
    modulus = 2 * seq_count * length_s
    slot_freq = row_order(seq_count)
    offsets = lax.axis_index("seq") * blk + jnp.arange(blk, dtype=jnp.int32)

    gated_rows = out_grad.astype(jnp.float32) * gate_act.astype(jnp.float32)
    gate_grad = (out_grad.astype(jnp.float32) * conv_out.astype(jnp.float32)).astype(jnp.bfloat16)
    stacked = jnp.concatenate(
        [
            gated_rows.reshape(row_total, length_s),
            value_act.astype(jnp.float32).reshape(row_total, length_s),
            filter_taps.reshape(1, length_s),
        ],
        axis=0,
    )
    recv1 = swap_leading(
        stacked.reshape(stack_rows, seq_count, sub, LANES).transpose(1, 0, 2, 3)
    )
    sources = jnp.arange(seq_count, dtype=jnp.int32)
    cross_re, cross_im = unit_table(sources[:, None] * sources[None, :], 2 * seq_count)
    half_re, _ = unit_table(sources * seq_count, 2 * seq_count)
    cross = jnp.stack(
        [cross_re, jnp.where((sources == 0)[:, None], half_re[None, :], cross_im)], axis=1
    ).reshape(2 * seq_count, seq_count)
    mixed = lmul(cross, recv1).reshape(seq_count, 2, stack_rows, sub, LANES)
    recv2 = swap_leading(mixed).transpose(0, 3, 1, 2, 4)
    dev = lax.axis_index("seq")
    is_first = dev == 0
    own_freq = (dev, jnp.where(is_first, seq_count, 2 * seq_count - dev))
    keep_im = jnp.where(is_first, 0.0, 1.0)
    coef = (
        ((1.0, 0.0), (0.0, keep_im)),
        ((keep_im, 0.0), (1.0 - keep_im, -keep_im)),
    )
    steps_a = jnp.arange(rows_a, dtype=jnp.int32)
    steps_b = jnp.arange(LANES, dtype=jnp.int32)
    lane_step = modulus // LANES
    parts = []
    for p in range(2):
        phase = (steps_a[:, None] * steps_a[None, :]) % LANES * lane_step + (
            LANES * own_freq[p] * steps_a[None, :]
        )
        t_re, t_im = unit_table(phase, modulus)
        for c in range(2):
            cols = []
            for q in range(2):
                k_re, k_im = coef[p][q]
                if c == 0:
                    cols.append(t_re * k_re - t_im * k_im)
                else:
                    cols.append(t_re * k_im + t_im * k_re)
            parts.append(jnp.stack(cols, axis=-1))
    block = jnp.stack(parts, axis=1).reshape(4 * rows_a, 2 * rows_a)
    y1 = lmul(block, recv2.reshape(2 * rows_a, stack_rows * LANES))
    y1 = y1.reshape(rows_a, 2, 2, stack_rows, LANES)
    y2_re = []
    y2_im = []
    for p in range(2):
        phase = steps_b[None, :] * own_freq[p] + steps_a[:, None] * steps_b[None, :] * (
            2 * seq_count
        )
        tw_re, tw_im = unit_table(phase, modulus)
        tw_re = tw_re[:, None, :]
        tw_im = tw_im[:, None, :]
        y1_re = y1[:, p, 0]
        y1_im = y1[:, p, 1]
        y2_re.append(y1_re * tw_re - y1_im * tw_im)
        y2_im.append(y1_re * tw_im + y1_im * tw_re)
    y2_re = jnp.stack(y2_re, axis=1)
    y2_im = jnp.stack(y2_im, axis=1)
    last_re, last_im = unit_table(steps_b[:, None] * steps_b[None, :], LANES)
    spec_re = rmul(y2_re, last_re) - rmul(y2_im, last_im)
    spec_im = rmul(y2_re, last_im) + rmul(y2_im, last_re)
    grad_re = spec_re[:, :, :row_total]
    grad_im = spec_im[:, :, :row_total]
    value_re = spec_re[:, :, row_total : 2 * row_total]
    value_im = spec_im[:, :, row_total : 2 * row_total]
    filt_re = spec_re[:, :, 2 * row_total :]
    filt_im = spec_im[:, :, 2 * row_total :]
    carry_re = filt_re * grad_re + filt_im * grad_im
    carry_im = filt_re * grad_im - filt_im * grad_re
    lag_re = jnp.sum(grad_re * value_re + grad_im * value_im, axis=2, keepdims=True)
    lag_im = jnp.sum(grad_im * value_re - grad_re * value_im, axis=2, keepdims=True)
    rows_time, lag_time = cross_inverse(
        *local_inverse(
            jnp.concatenate([carry_re, lag_re], axis=2),
            jnp.concatenate([carry_im, lag_im], axis=2),
            seq_count,
            slot_freq,
            offsets,
            modulus,
        ),
        seq_count,
    )
    inv_points = 1.0 / modulus
    carried = (rows_time * inv_points).reshape(batch_rows, channels, length_s)
    value_grad = (carried + skip_gain[None, :, None] * gated_rows).astype(jnp.bfloat16)
    norm_scale = 1.0 / math.sqrt(
        batch_rows * lax.axis_size("rep") * channels * length_s * seq_count
    )
    filter_grad = lag_time[0] * inv_points * norm_scale
    return (gate_grad, value_grad, filter_grad)


def solution(mesh):
    return jax.shard_map(
        local,
        mesh=mesh,
        in_specs=(
            P("rep", None, "seq"),
            P("rep", None, "seq"),
            P("rep", None, "seq"),
            P("rep", None, "seq"),
            P("seq"),
            P(),
        ),
        out_specs=(P("rep", None, "seq"), P("rep", None, "seq"), P("seq")),
        check_vma=False,
    )
```
